32 devices in a mesh: grp: 2 (over x), src: 16 (over z, y, core).
Axes of the slice: x: 2, y: 2, z: 4, core: 2. Of those that a mesh axis runs over, the one named last changes fastest.
Arguments:
- data_field: bfloat16 [2, 4096, 2048], P(None, ('grp', 'src')), parts along dimension 1, may hold values from -6 to 6
- primary_field: bfloat16 [2, 4096, 2048], P(None, ('grp', 'src')), parts along dimension 1, may hold values from -6 to 6
- station_weight: float32 [2048], replicated, may hold values from 0.25 to 4
- adaptive_filter: float32 [2, 4096], P(None, 'grp'), parts along dimension 1, may hold values from -1 to 1
Outputs:
- demultiple: float32 [2, 4096, 2048], P(None, ('grp', 'src')), parts along dimension 1
The draws below stay inside these ranges and needn't reach their ends.
There are 2 independent parts, one for each index of `grp`. The reference program is written for one: setup_inputs(seed, part) draws one part's arguments, and reference() takes and returns one part's arrays. A program takes and returns all parts, laid end to end along the dimension named above; an argument that names none is the same for every part. Nothing has to cross between parts.
All inputs are finite; a program needn't handle non-finite values.
Results may differ from the reference program's by a relative error of at most 0.008.
Values may be sent and summed in bfloat16 or wider, within the bound.
No kernel may reach another device: no remote copies, remote signals or barrier semaphores. Data moves between devices by JAX's collectives and lax.ppermute only.
A program may use at most 192 MiB of HBM per device.

```python
import math
import jax
import jax.numpy as jnp

N = 2048
ORDERS = 12


def draw_data_field(key, part):
    samples = jnp.clip(jax.random.normal(key, (2, N, N), jnp.float32), -6.0, 6.0)
    return samples.astype(jnp.bfloat16)


def shard_levels(key, dims, cuts, smallest, largest):
    def one(dim, shards_of):
        steps = jax.random.uniform(jax.random.fold_in(jax.random.fold_in(key, 6), dim), (shards_of,), jnp.float32, smallest / len(cuts), largest / len(cuts))
        return jnp.repeat(jnp.exp(steps), dims[dim] // shards_of).reshape((-1,) + (1,) * (len(dims) - dim - 1))

    factor_of = one(*cuts[0])
    for cut in cuts[1:]:
        factor_of = factor_of * one(*cut)
    return factor_of


def normal_values(own_key, extent, width, reach, pieces=(), kind=jnp.bfloat16):
    values = width * jax.random.normal(own_key, extent, jnp.float32)
    if pieces:
        values = values * shard_levels(own_key, extent, pieces, -0.22, 0.18)
    return jnp.clip(values, -reach, reach).astype(kind)


def setup_inputs(seed: int = 0, part: int = 0) -> dict:
    seeds = jax.random.split(jax.random.key(seed), 5)
    part_keys = jax.random.split(jax.random.fold_in(seeds[4], part), 5)
    data_field = draw_data_field(jax.random.fold_in(jax.random.fold_in(seeds[4], part), 71), part)
    primary_field = normal_values(part_keys[1], (2, N, N), 1.0, 6.0, ((1, 16),))
    station_weight = jnp.clip(jnp.exp(jax.random.uniform(seeds[2], (N,), jnp.float32, math.log(0.25), math.log(4.0))), 0.25, 4.0)
    adaptive_filter = jnp.clip(jax.random.uniform(part_keys[3], (2, N), jnp.float32, -1.0, 1.0), -1.0, 1.0)
    return {"data_field": data_field, "primary_field": primary_field, "station_weight": station_weight, "adaptive_filter": adaptive_filter}


def blend_rows(field, mirror, left_weight, right_weight):
    top = left_weight[:, None] * field.astype(jnp.float32) + right_weight[None, :] * mirror.astype(jnp.float32)
    return (top / (left_weight[:, None] + right_weight[None, :])).astype(jnp.bfloat16)

def reference(data_field, primary_field, station_weight, adaptive_filter):
    operator = blend_rows(data_field, data_field.transpose(0, 2, 1), station_weight, station_weight)
    factor = 0.8 / math.sqrt(N)
    current = primary_field
    prediction = jnp.zeros(data_field.shape, jnp.float32)
    for order in range(ORDERS):
        real_real = jnp.dot(current[0], operator[0], preferred_element_type=jnp.float32)
        imag_imag = jnp.dot(current[1], operator[1], preferred_element_type=jnp.float32)
        real_imag = jnp.dot(current[0], operator[1], preferred_element_type=jnp.float32)
        imag_real = jnp.dot(current[1], operator[0], preferred_element_type=jnp.float32)
        current = jnp.stack([(real_real - imag_imag) * factor, (real_imag + imag_real) * factor]).astype(jnp.bfloat16)
        prediction = prediction + current.astype(jnp.float32)
    filt_re = adaptive_filter[0][None, :]
    filt_im = adaptive_filter[1][None, :]
    out_re = data_field[0].astype(jnp.float32) - (filt_re * prediction[0] - filt_im * prediction[1])
    out_im = data_field[1].astype(jnp.float32) - (filt_re * prediction[1] + filt_im * prediction[0])
    return jnp.stack([out_re, out_im])
```

```python
import math

import numpy as np
import jax
import jax.numpy as jnp
from jax import lax
from jax.sharding import Mesh, PartitionSpec as P

ORDERS = 12
AXES = ("chip", "core")


def blend_rows(field, mirror, left_weight, right_weight):
    top = left_weight[:, None] * field.astype(jnp.float32) + right_weight[None, :] * mirror.astype(
        jnp.float32
    )
    return (top / (left_weight[:, None] + right_weight[None, :])).astype(jnp.bfloat16)


def upper_blocks(data_field, station_weight, parts, here):
    rows = data_field.shape[1]
    own_weight = lax.dynamic_slice_in_dim(station_weight, here * rows, rows)
    blocks = []
    for s in range(parts // 2 + 1):
        col = ((here + s) % parts) * rows
        own = lax.dynamic_slice_in_dim(data_field, col, rows, axis=2)
        if s == 0:
            mirror = own.swapaxes(1, 2)
        else:
            send = lax.dynamic_slice_in_dim(data_field, ((here - s) % parts) * rows, rows, axis=2)
            recv = lax.ppermute(send, AXES, perm=[(c, (c - s) % parts) for c in range(parts)])
            mirror = recv.swapaxes(1, 2)
        col_weight = lax.dynamic_slice_in_dim(station_weight, col, rows)
        blocks.append(blend_rows(own, mirror, own_weight, col_weight))
    return jnp.stack(blocks)


def assemble(gathered, chips, cores):
    parts = chips * cores
    slots = gathered.shape[2]
    rows = gathered.shape[-1]
    flat = gathered.reshape((parts, slots) + gathered.shape[3:])
    both = jnp.concatenate([flat, flat.swapaxes(-1, -2)], axis=1)
    where = lambda a: (a % cores) * chips + a // cores
    idx_a = np.zeros((parts, parts), np.int32)
    idx_s = np.zeros((parts, parts), np.int32)
    for r in range(parts):
        for c in range(parts):
            s = (c - r) % parts
            if s <= parts // 2:
                idx_a[r, c], idx_s[r, c] = where(r), s
            else:
                idx_a[r, c], idx_s[r, c] = where(c), slots + (r - c) % parts
    blocks = both[idx_a, idx_s]
    return blocks.transpose(2, 0, 3, 1, 4).reshape(2, parts * rows, parts * rows)


def local(data_field, primary_field, station_weight, adaptive_filter):
    rows = data_field.shape[1]
    order = data_field.shape[2]
    chips = lax.axis_size("chip")
    cores = lax.axis_size("core")
    parts = chips * cores
    here = lax.axis_index("chip") * cores + lax.axis_index("core")
    mine = upper_blocks(data_field, station_weight, parts, here)
    gathered = lax.all_gather(lax.all_gather(mine, "chip"), "core")
    operator = assemble(gathered, chips, cores)
    factor = 0.8 / math.sqrt(order)
    current = primary_field
    prediction = jnp.zeros(data_field.shape, jnp.float32)
    for step in range(ORDERS):
        stacked = current.reshape(2 * rows, order)
        with_real = jnp.dot(stacked, operator[0], preferred_element_type=jnp.float32)
        with_imag = jnp.dot(stacked, operator[1], preferred_element_type=jnp.float32)
        real_part = (with_real[:rows] - with_imag[rows:]) * factor
        imag_part = (with_imag[:rows] + with_real[rows:]) * factor
        current = jnp.stack([real_part, imag_part]).astype(jnp.bfloat16)
        prediction = prediction + current.astype(jnp.float32)
    filt_re = adaptive_filter[0][None, :]
    filt_im = adaptive_filter[1][None, :]
    out_re = data_field[0].astype(jnp.float32) - (filt_re * prediction[0] - filt_im * prediction[1])
    out_im = data_field[1].astype(jnp.float32) - (filt_re * prediction[1] + filt_im * prediction[0])
    return jnp.stack([out_re, out_im])


def solution(mesh):
    groups, parts = mesh.devices.shape
    split = Mesh(mesh.devices.reshape(groups, parts // 2, 2), ("grp",) + AXES)
    rows_spec = P(None, ("grp",) + AXES, None)
    return jax.shard_map(
        local,
        mesh=split,
        in_specs=(rows_spec, rows_spec, P(), P(None, "grp")),
        out_specs=rows_spec,
        check_vma=False,
    )
```

```python
import math

import numpy as np
import jax
import jax.numpy as jnp
from jax import lax
from jax.experimental import pallas as pl
from jax.experimental.pallas import tpu as pltpu
from jax.sharding import Mesh, PartitionSpec as P

ORDERS = 12
AXES = ("chip", "core")


def blend_rows(field, mirror, left_weight, right_weight):
    top = left_weight[:, None] * field.astype(jnp.float32) + right_weight[None, :] * mirror.astype(
        jnp.float32
    )
    return (top / (left_weight[:, None] + right_weight[None, :])).astype(jnp.bfloat16)


def upper_blocks(data_field, station_weight, parts, here):
    rows = data_field.shape[1]
    own_weight = lax.dynamic_slice_in_dim(station_weight, here * rows, rows)
    blocks = []
    for s in range(parts // 2 + 1):
        col = ((here + s) % parts) * rows
        own = lax.dynamic_slice_in_dim(data_field, col, rows, axis=2)
        if s == 0:
            mirror = own.swapaxes(1, 2)
        else:
            send = lax.dynamic_slice_in_dim(data_field, ((here - s) % parts) * rows, rows, axis=2)
            recv = lax.ppermute(send, AXES, perm=[(c, (c - s) % parts) for c in range(parts)])
            mirror = recv.swapaxes(1, 2)
        col_weight = lax.dynamic_slice_in_dim(station_weight, col, rows)
        blocks.append(blend_rows(own, mirror, own_weight, col_weight))
    return jnp.stack(blocks)


def assemble(gathered, chips, cores):
    parts = chips * cores
    slots = gathered.shape[2]
    rows = gathered.shape[-1]
    flat = gathered.reshape((parts, slots) + gathered.shape[3:])
    both = jnp.concatenate([flat, flat.swapaxes(-1, -2)], axis=1)
    where = lambda a: (a % cores) * chips + a // cores
    idx_a = np.zeros((parts, parts), np.int32)
    idx_s = np.zeros((parts, parts), np.int32)
    for r in range(parts):
        for c in range(parts):
            s = (c - r) % parts
            if s <= parts // 2:
                idx_a[r, c], idx_s[r, c] = where(r), s
            else:
                idx_a[r, c], idx_s[r, c] = where(c), slots + (r - c) % parts
    blocks = both[idx_a, idx_s]
    return blocks.transpose(2, 0, 3, 1, 4).reshape(2, parts * rows, parts * rows)


def assemble_kernel(g_ref, re_ref, im_ref, buf, sem):
    cores, chips, slots, _, rows, _ = g_ref.shape
    parts = chips * cores
    r = pl.program_id(0)
    copies = []
    for c in range(parts):
        s = (c - r + parts) % parts
        up = s <= parts // 2
        a = jnp.where(up, r, c)
        src = g_ref.at[a % cores, a // cores, jnp.where(up, s, parts - s)]
        copy = pltpu.make_async_copy(src, buf.at[c], sem.at[c])
        copy.start()
        copies.append(copy)
    for c in range(parts):
        copies[c].wait()
        s = (c - r + parts) % parts
        up = s <= parts // 2
        for k, out in ((0, re_ref), (1, im_ref)):
            block = buf[c, k]

            @pl.when(up)
            def _():
                out[:, c * rows:(c + 1) * rows] = block

            @pl.when(jnp.logical_not(up))
            def _():
                out[:, c * rows:(c + 1) * rows] = block.astype(jnp.float32).T.astype(jnp.bfloat16)


def assemble_pallas(gathered, chips, cores):
    parts = chips * cores
    rows = gathered.shape[-1]
    order = parts * rows
    return pl.pallas_call(
        assemble_kernel,
        grid=(parts,),
        in_specs=[pl.BlockSpec(memory_space=pl.ANY)],
        out_specs=[pl.BlockSpec((rows, order), lambda r: (r, 0))] * 2,
        out_shape=[jax.ShapeDtypeStruct((order, order), jnp.bfloat16)] * 2,
        scratch_shapes=[pltpu.VMEM((parts, 2, rows, rows), jnp.bfloat16), pltpu.SemaphoreType.DMA((parts,))],
    )(gathered)


def local(data_field, primary_field, station_weight, adaptive_filter):
    rows = data_field.shape[1]
    order = data_field.shape[2]
    chips = lax.axis_size("chip")
    cores = lax.axis_size("core")
    parts = chips * cores
    here = lax.axis_index("chip") * cores + lax.axis_index("core")
    mine = upper_blocks(data_field, station_weight, parts, here)
    gathered = lax.all_gather(lax.all_gather(mine, "chip"), "core")
    if rows % 128 == 0:
        operator = assemble_pallas(gathered, chips, cores)
    else:
        operator = assemble(gathered, chips, cores)
    factor = 0.8 / math.sqrt(order)
    current = primary_field
    prediction = jnp.zeros(data_field.shape, jnp.float32)
    for step in range(ORDERS):
        stacked = current.reshape(2 * rows, order)
        with_real = jnp.dot(stacked, operator[0], preferred_element_type=jnp.float32)
        with_imag = jnp.dot(stacked, operator[1], preferred_element_type=jnp.float32)
        real_part = (with_real[:rows] - with_imag[rows:]) * factor
        imag_part = (with_imag[:rows] + with_real[rows:]) * factor
        current = jnp.stack([real_part, imag_part]).astype(jnp.bfloat16)
        prediction = prediction + current.astype(jnp.float32)
    filt_re = adaptive_filter[0][None, :]
    filt_im = adaptive_filter[1][None, :]
    out_re = data_field[0].astype(jnp.float32) - (filt_re * prediction[0] - filt_im * prediction[1])
    out_im = data_field[1].astype(jnp.float32) - (filt_re * prediction[1] + filt_im * prediction[0])
    return jnp.stack([out_re, out_im])


def solution(mesh):
    groups, parts = mesh.devices.shape
    split = Mesh(mesh.devices.reshape(groups, parts // 2, 2), ("grp",) + AXES)
    rows_spec = P(None, ("grp",) + AXES, None)
    return jax.shard_map(
        local,
        mesh=split,
        in_specs=(rows_spec, rows_spec, P(), P(None, "grp")),
        out_specs=rows_spec,
        check_vma=False,
    )
```

```python
import math

import numpy as np
import jax
import jax.numpy as jnp
from jax import lax
from jax.experimental import pallas as pl
from jax.experimental.pallas import tpu as pltpu
from jax.sharding import Mesh, PartitionSpec as P

ORDERS = 12
AXES = ("chip", "core")


def blend_rows(field, mirror, left_weight, right_weight):
    top = left_weight[:, None] * field.astype(jnp.float32) + right_weight[None, :] * mirror.astype(
        jnp.float32
    )
    return (top / (left_weight[:, None] + right_weight[None, :])).astype(jnp.bfloat16)


def upper_blocks(data_field, station_weight, parts, here):
    rows = data_field.shape[1]
    own_weight = lax.dynamic_slice_in_dim(station_weight, here * rows, rows)
    blocks = []
    for s in range(parts // 2 + 1):
        col = ((here + s) % parts) * rows
        own = lax.dynamic_slice_in_dim(data_field, col, rows, axis=2)
        if s == 0:
            mirror = own.swapaxes(1, 2)
        else:
            send = lax.dynamic_slice_in_dim(data_field, ((here - s) % parts) * rows, rows, axis=2)
            recv = lax.ppermute(send, AXES, perm=[(c, (c - s) % parts) for c in range(parts)])
            mirror = recv.swapaxes(1, 2)
        col_weight = lax.dynamic_slice_in_dim(station_weight, col, rows)
        blocks.append(blend_rows(own, mirror, own_weight, col_weight))
    return jnp.stack(blocks)


def assemble(gathered, chips, cores):
    parts = chips * cores
    slots = gathered.shape[2]
    rows = gathered.shape[-1]
    flat = gathered.reshape((parts, slots) + gathered.shape[3:])
    both = jnp.concatenate([flat, flat.swapaxes(-1, -2)], axis=1)
    where = lambda a: (a % cores) * chips + a // cores
    idx_a = np.zeros((parts, parts), np.int32)
    idx_s = np.zeros((parts, parts), np.int32)
    for r in range(parts):
        for c in range(parts):
            s = (c - r) % parts
            if s <= parts // 2:
                idx_a[r, c], idx_s[r, c] = where(r), s
            else:
                idx_a[r, c], idx_s[r, c] = where(c), slots + (r - c) % parts
    blocks = both[idx_a, idx_s]
    return blocks.transpose(2, 0, 3, 1, 4).reshape(2, parts * rows, parts * rows)


def assemble_kernel(g_ref, re_ref, im_ref, buf, sem):
    cores, chips, slots, _, rows, _ = g_ref.shape
    parts = chips * cores
    r = pl.program_id(0)

    def copies(row, slot):
        out = []
        for c in range(parts):
            s = (c - row + parts) % parts
            up = s <= parts // 2
            a = jnp.where(up, row, c)
            src = g_ref.at[a % cores, a // cores, jnp.where(up, s, parts - s)]
            out.append(pltpu.make_async_copy(src, buf.at[slot, c], sem.at[slot, c]))
        return out

    @pl.when(r == 0)
    def _():
        for copy in copies(r, 0):
            copy.start()

    @pl.when(r + 1 < parts)
    def _():
        for copy in copies(r + 1, (r + 1) % 2):
            copy.start()

    slot = r % 2
    eye = (lax.broadcasted_iota(jnp.int32, (rows, rows), 0) == lax.broadcasted_iota(jnp.int32, (rows, rows), 1)).astype(jnp.bfloat16)
    for c, copy in enumerate(copies(r, slot)):
        copy.wait()
        s = (c - r + parts) % parts
        up = s <= parts // 2
        for k, out in ((0, re_ref), (1, im_ref)):
            block = buf[slot, c, k]

            @pl.when(up)
            def _():
                out[:, c * rows:(c + 1) * rows] = block

            @pl.when(jnp.logical_not(up))
            def _():
                flipped = lax.dot_general(eye, block, (((1,), (1,)), ((), ())), preferred_element_type=jnp.float32)
                out[:, c * rows:(c + 1) * rows] = flipped.astype(jnp.bfloat16)


def assemble_pallas(gathered, chips, cores):
    parts = chips * cores
    rows = gathered.shape[-1]
    order = parts * rows
    return pl.pallas_call(
        assemble_kernel,
        grid=(parts,),
        in_specs=[pl.BlockSpec(memory_space=pl.ANY)],
        out_specs=[pl.BlockSpec((rows, order), lambda r: (r, 0))] * 2,
        out_shape=[jax.ShapeDtypeStruct((order, order), jnp.bfloat16)] * 2,
        scratch_shapes=[pltpu.VMEM((2, parts, 2, rows, rows), jnp.bfloat16), pltpu.SemaphoreType.DMA((2, parts))],
        compiler_params=pltpu.CompilerParams(dimension_semantics=("arbitrary",)),
    )(gathered)


def local(data_field, primary_field, station_weight, adaptive_filter):
    rows = data_field.shape[1]
    order = data_field.shape[2]
    chips = lax.axis_size("chip")
    cores = lax.axis_size("core")
    parts = chips * cores
    here = lax.axis_index("chip") * cores + lax.axis_index("core")
    mine = upper_blocks(data_field, station_weight, parts, here)
    gathered = lax.all_gather(mine, AXES)[None]
    if rows % 128 == 0:
        operator = assemble_pallas(gathered, parts, 1)
    else:
        operator = assemble(gathered, parts, 1)
    factor = 0.8 / math.sqrt(order)
    current = primary_field
    prediction = jnp.zeros(data_field.shape, jnp.float32)
    for step in range(ORDERS):
        stacked = current.reshape(2 * rows, order)
        with_real = jnp.dot(stacked, operator[0], preferred_element_type=jnp.float32)
        with_imag = jnp.dot(stacked, operator[1], preferred_element_type=jnp.float32)
        real_part = (with_real[:rows] - with_imag[rows:]) * factor
        imag_part = (with_imag[:rows] + with_real[rows:]) * factor
        current = jnp.stack([real_part, imag_part]).astype(jnp.bfloat16)
        prediction = prediction + current.astype(jnp.float32)
    filt_re = adaptive_filter[0][None, :]
    filt_im = adaptive_filter[1][None, :]
    out_re = data_field[0].astype(jnp.float32) - (filt_re * prediction[0] - filt_im * prediction[1])
    out_im = data_field[1].astype(jnp.float32) - (filt_re * prediction[1] + filt_im * prediction[0])
    return jnp.stack([out_re, out_im])


def solution(mesh):
    groups, parts = mesh.devices.shape
    split = Mesh(mesh.devices.reshape(groups, parts // 2, 2), ("grp",) + AXES)
    rows_spec = P(None, ("grp",) + AXES, None)
    return jax.shard_map(
        local,
        mesh=split,
        in_specs=(rows_spec, rows_spec, P(), P(None, "grp")),
        out_specs=rows_spec,
        check_vma=False,
    )
```

```python
import math

import numpy as np
import jax
import jax.numpy as jnp
from jax import lax
from jax.experimental import pallas as pl
from jax.experimental.pallas import tpu as pltpu
from jax.sharding import Mesh, PartitionSpec as P

ORDERS = 12
AXES = ("chip", "core")


def blend_rows(field, mirror, left_weight, right_weight):
    top = left_weight[:, None] * field.astype(jnp.float32) + right_weight[None, :] * mirror.astype(
        jnp.float32
    )
    return (top / (left_weight[:, None] + right_weight[None, :])).astype(jnp.bfloat16)


def upper_blocks(data_field, station_weight, parts, here):
    rows = data_field.shape[1]
    own_weight = lax.dynamic_slice_in_dim(station_weight, here * rows, rows)
    blocks = []
    for s in range(parts // 2 + 1):
        col = ((here + s) % parts) * rows
        own = lax.dynamic_slice_in_dim(data_field, col, rows, axis=2)
        if s == 0:
            mirror = own.swapaxes(1, 2)
        else:
            send = lax.dynamic_slice_in_dim(data_field, ((here - s) % parts) * rows, rows, axis=2)
            recv = lax.ppermute(send, AXES, perm=[(c, (c - s) % parts) for c in range(parts)])
            mirror = recv.swapaxes(1, 2)
        col_weight = lax.dynamic_slice_in_dim(station_weight, col, rows)
        blocks.append(blend_rows(own, mirror, own_weight, col_weight))
    return jnp.stack(blocks)


def assemble(gathered, chips, cores):
    parts = chips * cores
    slots = gathered.shape[2]
    rows = gathered.shape[-1]
    flat = gathered.reshape((parts, slots) + gathered.shape[3:])
    both = jnp.concatenate([flat, flat.swapaxes(-1, -2)], axis=1)
    where = lambda a: (a % cores) * chips + a // cores
    idx_a = np.zeros((parts, parts), np.int32)
    idx_s = np.zeros((parts, parts), np.int32)
    for r in range(parts):
        for c in range(parts):
            s = (c - r) % parts
            if s <= parts // 2:
                idx_a[r, c], idx_s[r, c] = where(r), s
            else:
                idx_a[r, c], idx_s[r, c] = where(c), slots + (r - c) % parts
    blocks = both[idx_a, idx_s]
    return blocks.transpose(2, 0, 3, 1, 4).reshape(2, parts * rows, parts * rows)


def assemble_kernel(g_ref, re_ref, im_ref, upper, lower, sem):
    cores, chips, slots, _, rows, _ = g_ref.shape
    parts = chips * cores
    r = pl.program_id(0)

    def copies(row, slot):
        out = [pltpu.make_async_copy(g_ref.at[row % cores, row // cores], upper.at[slot], sem.at[slot, 0])]
        for t in range(1, parts // 2):
            a = (row + parts - t) % parts
            out.append(pltpu.make_async_copy(g_ref.at[a % cores, a // cores, t], lower.at[slot, t], sem.at[slot, t]))
        return out

    @pl.when(r == 0)
    def _():
        for copy in copies(r, 0):
            copy.start()

    @pl.when(r + 1 < parts)
    def _():
        for copy in copies(r + 1, (r + 1) % 2):
            copy.start()

    slot = r % 2
    for copy in copies(r, slot):
        copy.wait()
    for s in range(parts):
        col = pl.multiple_of(((r + s) % parts) * rows, rows)
        for k, out in ((0, re_ref), (1, im_ref)):
            if s <= parts // 2:
                block = upper[slot, s, k]
            else:
                block = lower[slot, parts - s, k].astype(jnp.float32).T.astype(jnp.bfloat16)
            out[:, pl.ds(col, rows)] = block


def assemble_pallas(gathered, chips, cores):
    parts = chips * cores
    rows = gathered.shape[-1]
    order = parts * rows
    return pl.pallas_call(
        assemble_kernel,
        grid=(parts,),
        in_specs=[pl.BlockSpec(memory_space=pl.ANY)],
        out_specs=[pl.BlockSpec((rows, order), lambda r: (r, 0))] * 2,
        out_shape=[jax.ShapeDtypeStruct((order, order), jnp.bfloat16)] * 2,
        scratch_shapes=[
            pltpu.VMEM((2, gathered.shape[2], 2, rows, rows), jnp.bfloat16),
            pltpu.VMEM((2, parts // 2, 2, rows, rows), jnp.bfloat16),
            pltpu.SemaphoreType.DMA((2, parts // 2)),
        ],
        compiler_params=pltpu.CompilerParams(dimension_semantics=("arbitrary",)),
    )(gathered)


def local(data_field, primary_field, station_weight, adaptive_filter):
    rows = data_field.shape[1]
    order = data_field.shape[2]
    chips = lax.axis_size("chip")
    cores = lax.axis_size("core")
    parts = chips * cores
    here = lax.axis_index("chip") * cores + lax.axis_index("core")
    mine = upper_blocks(data_field, station_weight, parts, here)
    gathered = lax.all_gather(mine, AXES)[None]
    if rows % 128 == 0:
        operator = assemble_pallas(gathered, parts, 1)
    else:
        operator = assemble(gathered, parts, 1)
    factor = 0.8 / math.sqrt(order)
    current = primary_field
    prediction = jnp.zeros(data_field.shape, jnp.float32)
    for step in range(ORDERS):
        stacked = current.reshape(2 * rows, order)
        with_real = jnp.dot(stacked, operator[0], preferred_element_type=jnp.float32)
        with_imag = jnp.dot(stacked, operator[1], preferred_element_type=jnp.float32)
        real_part = (with_real[:rows] - with_imag[rows:]) * factor
        imag_part = (with_imag[:rows] + with_real[rows:]) * factor
        current = jnp.stack([real_part, imag_part]).astype(jnp.bfloat16)
        prediction = prediction + current.astype(jnp.float32)
    filt_re = adaptive_filter[0][None, :]
    filt_im = adaptive_filter[1][None, :]
    out_re = data_field[0].astype(jnp.float32) - (filt_re * prediction[0] - filt_im * prediction[1])
    out_im = data_field[1].astype(jnp.float32) - (filt_re * prediction[1] + filt_im * prediction[0])
    return jnp.stack([out_re, out_im])


def solution(mesh):
    groups, parts = mesh.devices.shape
    split = Mesh(mesh.devices.reshape(groups, parts // 2, 2), ("grp",) + AXES)
    rows_spec = P(None, ("grp",) + AXES, None)
    return jax.shard_map(
        local,
        mesh=split,
        in_specs=(rows_spec, rows_spec, P(), P(None, "grp")),
        out_specs=rows_spec,
        check_vma=False,
    )
```

```python
import math

import numpy as np
import jax
import jax.numpy as jnp
from jax import lax
from jax.experimental import pallas as pl
from jax.experimental.pallas import tpu as pltpu
from jax.sharding import Mesh, PartitionSpec as P

ORDERS = 12
AXES = ("chip", "core")


def blend_rows(field, mirror, left_weight, right_weight):
    top = left_weight[:, None] * field.astype(jnp.float32) + right_weight[None, :] * mirror.astype(
        jnp.float32
    )
    return (top / (left_weight[:, None] + right_weight[None, :])).astype(jnp.bfloat16)


def upper_blocks(data_field, station_weight, parts, here):
    rows = data_field.shape[1]
    half = parts // 2
    rolled = jnp.roll(data_field.reshape(2, rows, parts, rows), -here, axis=2)
    own = rolled[:, :, : half + 1]
    received = [rolled[:, :, 0]]
    for s in range(1, half + 1):
        perm = [(c, (c - s) % parts) for c in range(parts)]
        received.append(lax.ppermute(rolled[:, :, parts - s], AXES, perm=perm))
    mirror = jnp.stack(received, axis=2).transpose(0, 3, 2, 1)
    own_weight = lax.dynamic_slice_in_dim(station_weight, here * rows, rows)[:, None, None]
    col_weight = jnp.roll(station_weight.reshape(parts, rows), -here, axis=0)[None, : half + 1]
    top = own_weight * own.astype(jnp.float32) + col_weight * mirror.astype(jnp.float32)
    blended = (top / (own_weight + col_weight)).astype(jnp.bfloat16)
    return blended.transpose(2, 0, 1, 3)


def assemble(gathered, chips, cores):
    parts = chips * cores
    slots = gathered.shape[2]
    rows = gathered.shape[-1]
    flat = gathered.reshape((parts, slots) + gathered.shape[3:])
    both = jnp.concatenate([flat, flat.swapaxes(-1, -2)], axis=1)
    where = lambda a: (a % cores) * chips + a // cores
    idx_a = np.zeros((parts, parts), np.int32)
    idx_s = np.zeros((parts, parts), np.int32)
    for r in range(parts):
        for c in range(parts):
            s = (c - r) % parts
            if s <= parts // 2:
                idx_a[r, c], idx_s[r, c] = where(r), s
            else:
                idx_a[r, c], idx_s[r, c] = where(c), slots + (r - c) % parts
    blocks = both[idx_a, idx_s]
    return blocks.transpose(2, 0, 3, 1, 4).reshape(2, parts * rows, parts * rows)


def assemble_kernel(g_ref, re_ref, im_ref, upper, lower, sem):
    cores, chips, slots, _, rows, _ = g_ref.shape
    parts = chips * cores
    r = pl.program_id(0)

    def copies(row, slot):
        out = [pltpu.make_async_copy(g_ref.at[row % cores, row // cores], upper.at[slot], sem.at[slot, 0])]
        for t in range(1, parts // 2):
            a = (row + parts - t) % parts
            out.append(pltpu.make_async_copy(g_ref.at[a % cores, a // cores, t], lower.at[slot, t], sem.at[slot, t]))
        return out

    @pl.when(r == 0)
    def _():
        for copy in copies(r, 0):
            copy.start()

    @pl.when(r + 1 < parts)
    def _():
        for copy in copies(r + 1, (r + 1) % 2):
            copy.start()

    slot = r % 2
    for copy in copies(r, slot):
        copy.wait()
    for s in range(parts):
        col = pl.multiple_of(((r + s) % parts) * rows, rows)
        for k, out in ((0, re_ref), (1, im_ref)):
            if s <= parts // 2:
                block = upper[slot, s, k]
            else:
                block = lower[slot, parts - s, k].astype(jnp.float32).T.astype(jnp.bfloat16)
            out[:, pl.ds(col, rows)] = block


def assemble_pallas(gathered, chips, cores):
    parts = chips * cores
    rows = gathered.shape[-1]
    order = parts * rows
    return pl.pallas_call(
        assemble_kernel,
        grid=(parts,),
        in_specs=[pl.BlockSpec(memory_space=pl.ANY)],
        out_specs=[pl.BlockSpec((rows, order), lambda r: (r, 0))] * 2,
        out_shape=[jax.ShapeDtypeStruct((order, order), jnp.bfloat16)] * 2,
        scratch_shapes=[
            pltpu.VMEM((2, gathered.shape[2], 2, rows, rows), jnp.bfloat16),
            pltpu.VMEM((2, parts // 2, 2, rows, rows), jnp.bfloat16),
            pltpu.SemaphoreType.DMA((2, parts // 2)),
        ],
        compiler_params=pltpu.CompilerParams(dimension_semantics=("arbitrary",)),
    )(gathered)


def local(data_field, primary_field, station_weight, adaptive_filter):
    rows = data_field.shape[1]
    order = data_field.shape[2]
    chips = lax.axis_size("chip")
    cores = lax.axis_size("core")
    parts = chips * cores
    here = lax.axis_index("chip") * cores + lax.axis_index("core")
    mine = upper_blocks(data_field, station_weight, parts, here)
    gathered = lax.all_gather(mine, AXES)[None]
    if rows % 128 == 0:
        operator = assemble_pallas(gathered, parts, 1)
    else:
        operator = assemble(gathered, parts, 1)
    factor = 0.8 / math.sqrt(order)
    current = primary_field
    prediction = jnp.zeros(data_field.shape, jnp.float32)
    for step in range(ORDERS):
        stacked = current.reshape(2 * rows, order)
        with_real = jnp.dot(stacked, operator[0], preferred_element_type=jnp.float32)
        with_imag = jnp.dot(stacked, operator[1], preferred_element_type=jnp.float32)
        real_part = (with_real[:rows] - with_imag[rows:]) * factor
        imag_part = (with_imag[:rows] + with_real[rows:]) * factor
        current = jnp.stack([real_part, imag_part]).astype(jnp.bfloat16)
        prediction = prediction + current.astype(jnp.float32)
    filt_re = adaptive_filter[0][None, :]
    filt_im = adaptive_filter[1][None, :]
    out_re = data_field[0].astype(jnp.float32) - (filt_re * prediction[0] - filt_im * prediction[1])
    out_im = data_field[1].astype(jnp.float32) - (filt_re * prediction[1] + filt_im * prediction[0])
    return jnp.stack([out_re, out_im])


def solution(mesh):
    groups, parts = mesh.devices.shape
    split = Mesh(mesh.devices.reshape(groups, parts // 2, 2), ("grp",) + AXES)
    rows_spec = P(None, ("grp",) + AXES, None)
    return jax.shard_map(
        local,
        mesh=split,
        in_specs=(rows_spec, rows_spec, P(), P(None, "grp")),
        out_specs=rows_spec,
        check_vma=False,
    )
```

```python
import math

import numpy as np
import jax
import jax.numpy as jnp
from jax import lax
from jax.experimental import pallas as pl
from jax.experimental.pallas import tpu as pltpu
from jax.sharding import Mesh, PartitionSpec as P

ORDERS = 12
AXES = ("chip", "core")


def blend_rows(field, mirror, left_weight, right_weight):
    top = left_weight[:, None] * field.astype(jnp.float32) + right_weight[None, :] * mirror.astype(
        jnp.float32
    )
    return (top / (left_weight[:, None] + right_weight[None, :])).astype(jnp.bfloat16)


def upper_blocks(data_field, station_weight, parts, here):
    rows = data_field.shape[1]
    half = parts // 2
    rolled = jnp.roll(data_field.reshape(2, rows, parts, rows), -here, axis=2)
    own = rolled[:, :, : half + 1]
    received = [rolled[:, :, 0]]
    for s in range(1, half + 1):
        perm = [(c, (c - s) % parts) for c in range(parts)]
        received.append(lax.ppermute(rolled[:, :, parts - s], AXES, perm=perm))
    own_weight = lax.dynamic_slice_in_dim(station_weight, here * rows, rows)[:, None, None]
    col_weight = jnp.roll(station_weight.reshape(parts, rows), -here, axis=0)[None, : half + 1]
    chunks = []
    for lo, hi in chunk_bounds(half + 1):
        mirror = jnp.stack(received[lo:hi], axis=2).transpose(0, 3, 2, 1)
        top = own_weight * own[:, :, lo:hi].astype(jnp.float32) + col_weight[:, lo:hi] * mirror.astype(jnp.float32)
        blended = (top / (own_weight + col_weight[:, lo:hi])).astype(jnp.bfloat16)
        chunks.append(blended.transpose(2, 0, 1, 3))
    return chunks


def chunk_bounds(slots, pieces=3):
    edges = [round(i * slots / pieces) for i in range(pieces + 1)]
    return list(zip(edges[:-1], edges[1:]))


def assemble(gathered, chips, cores):
    parts = chips * cores
    slots = gathered.shape[2]
    rows = gathered.shape[-1]
    flat = gathered.reshape((parts, slots) + gathered.shape[3:])
    both = jnp.concatenate([flat, flat.swapaxes(-1, -2)], axis=1)
    where = lambda a: (a % cores) * chips + a // cores
    idx_a = np.zeros((parts, parts), np.int32)
    idx_s = np.zeros((parts, parts), np.int32)
    for r in range(parts):
        for c in range(parts):
            s = (c - r) % parts
            if s <= parts // 2:
                idx_a[r, c], idx_s[r, c] = where(r), s
            else:
                idx_a[r, c], idx_s[r, c] = where(c), slots + (r - c) % parts
    blocks = both[idx_a, idx_s]
    return blocks.transpose(2, 0, 3, 1, 4).reshape(2, parts * rows, parts * rows)


def assemble_kernel(*refs):
    pieces = len(refs) - 5
    g_refs, (re_ref, im_ref, upper, lower, sem) = refs[:pieces], refs[pieces:]
    parts = g_refs[0].shape[0]
    rows = g_refs[0].shape[-1]
    bounds = chunk_bounds(parts // 2 + 1, pieces)
    r = pl.program_id(0)

    def copies(row, slot):
        out = []
        for k, (lo, hi) in enumerate(bounds):
            out.append(pltpu.make_async_copy(g_refs[k].at[row], upper.at[slot, pl.ds(lo, hi - lo)], sem.at[slot, k]))
        for t in range(1, parts // 2):
            a = (row + parts - t) % parts
            k = [k for k, (lo, hi) in enumerate(bounds) if lo <= t < hi][0]
            src = g_refs[k].at[a, t - bounds[k][0]]
            out.append(pltpu.make_async_copy(src, lower.at[slot, t], sem.at[slot, pieces + t]))
        return out

    @pl.when(r == 0)
    def _():
        for copy in copies(r, 0):
            copy.start()

    @pl.when(r + 1 < parts)
    def _():
        for copy in copies(r + 1, (r + 1) % 2):
            copy.start()

    slot = r % 2
    for copy in copies(r, slot):
        copy.wait()
    for s in range(parts):
        col = pl.multiple_of(((r + s) % parts) * rows, rows)
        for k, out in ((0, re_ref), (1, im_ref)):
            if s <= parts // 2:
                block = upper[slot, s, k]
            else:
                block = lower[slot, parts - s, k].astype(jnp.float32).T.astype(jnp.bfloat16)
            out[:, pl.ds(col, rows)] = block


def assemble_pallas(chunks):
    parts = chunks[0].shape[0]
    rows = chunks[0].shape[-1]
    slots = sum(c.shape[1] for c in chunks)
    order = parts * rows
    return pl.pallas_call(
        assemble_kernel,
        grid=(parts,),
        in_specs=[pl.BlockSpec(memory_space=pl.ANY)] * len(chunks),
        out_specs=[pl.BlockSpec((rows, order), lambda r: (r, 0))] * 2,
        out_shape=[jax.ShapeDtypeStruct((order, order), jnp.bfloat16)] * 2,
        scratch_shapes=[
            pltpu.VMEM((2, slots, 2, rows, rows), jnp.bfloat16),
            pltpu.VMEM((2, parts // 2, 2, rows, rows), jnp.bfloat16),
            pltpu.SemaphoreType.DMA((2, len(chunks) + parts // 2)),
        ],
        compiler_params=pltpu.CompilerParams(dimension_semantics=("arbitrary",)),
    )(*chunks)


def local(data_field, primary_field, station_weight, adaptive_filter):
    rows = data_field.shape[1]
    order = data_field.shape[2]
    chips = lax.axis_size("chip")
    cores = lax.axis_size("core")
    parts = chips * cores
    here = lax.axis_index("chip") * cores + lax.axis_index("core")
    pieces = upper_blocks(data_field, station_weight, parts, here)
    gathered = [lax.all_gather(jnp.concatenate(pieces, axis=0), AXES)]
    if rows % 128 == 0:
        operator = assemble_pallas(gathered)
    else:
        operator = assemble(jnp.concatenate(gathered, axis=1)[None], parts, 1)
    factor = 0.8 / math.sqrt(order)

    def step(_, carry):
        current, prediction = carry
        stacked = current.reshape(2 * rows, order)
        with_real = jnp.dot(stacked, operator[0], preferred_element_type=jnp.float32)
        with_imag = jnp.dot(stacked, operator[1], preferred_element_type=jnp.float32)
        real_part = (with_real[:rows] - with_imag[rows:]) * factor
        imag_part = (with_imag[:rows] + with_real[rows:]) * factor
        current = jnp.stack([real_part, imag_part]).astype(jnp.bfloat16)
        return current, prediction + current.astype(jnp.float32)

    current, prediction = lax.fori_loop(0, ORDERS, step, (primary_field, jnp.zeros(data_field.shape, jnp.float32)))
    filt_re = adaptive_filter[0][None, :]
    filt_im = adaptive_filter[1][None, :]
    out_re = data_field[0].astype(jnp.float32) - (filt_re * prediction[0] - filt_im * prediction[1])
    out_im = data_field[1].astype(jnp.float32) - (filt_re * prediction[1] + filt_im * prediction[0])
    return jnp.stack([out_re, out_im])


def solution(mesh):
    groups, parts = mesh.devices.shape
    split = Mesh(mesh.devices.reshape(groups, parts // 2, 2), ("grp",) + AXES)
    rows_spec = P(None, ("grp",) + AXES, None)
    return jax.shard_map(
        local,
        mesh=split,
        in_specs=(rows_spec, rows_spec, P(), P(None, "grp")),
        out_specs=rows_spec,
        check_vma=False,
    )
```

```python
import functools
import math

import numpy as np
import jax
import jax.numpy as jnp
from jax import lax
from jax.experimental import pallas as pl
from jax.experimental.pallas import tpu as pltpu
from jax.sharding import Mesh, PartitionSpec as P

ORDERS = 12
AXES = ("chip", "core")


def blend_rows(field, mirror, left_weight, right_weight):
    top = left_weight[:, None] * field.astype(jnp.float32) + right_weight[None, :] * mirror.astype(
        jnp.float32
    )
    return (top / (left_weight[:, None] + right_weight[None, :])).astype(jnp.bfloat16)


def upper_blocks(data_field, station_weight, parts, here):
    rows = data_field.shape[1]
    half = parts // 2
    rolled = jnp.roll(data_field.reshape(2, rows, parts, rows), -here, axis=2)
    own = rolled[:, :, : half + 1]
    received = [rolled[:, :, 0]]
    for s in range(1, half + 1):
        perm = [(c, (c - s) % parts) for c in range(parts)]
        received.append(lax.ppermute(rolled[:, :, parts - s], AXES, perm=perm))
    own_weight = lax.dynamic_slice_in_dim(station_weight, here * rows, rows)[:, None, None]
    col_weight = jnp.roll(station_weight.reshape(parts, rows), -here, axis=0)[None, : half + 1]
    chunks = []
    for lo, hi in chunk_bounds(half + 1):
        mirror = jnp.stack(received[lo:hi], axis=2).transpose(0, 3, 2, 1)
        top = own_weight * own[:, :, lo:hi].astype(jnp.float32) + col_weight[:, lo:hi] * mirror.astype(jnp.float32)
        blended = (top / (own_weight + col_weight[:, lo:hi])).astype(jnp.bfloat16)
        chunks.append(blended.transpose(2, 0, 1, 3))
    return chunks


def chunk_bounds(slots, pieces=3):
    edges = [round(i * slots / pieces) for i in range(pieces + 1)]
    return list(zip(edges[:-1], edges[1:]))


def assemble(gathered, chips, cores):
    parts = chips * cores
    slots = gathered.shape[2]
    rows = gathered.shape[-1]
    flat = gathered.reshape((parts, slots) + gathered.shape[3:])
    both = jnp.concatenate([flat, flat.swapaxes(-1, -2)], axis=1)
    where = lambda a: (a % cores) * chips + a // cores
    idx_a = np.zeros((parts, parts), np.int32)
    idx_s = np.zeros((parts, parts), np.int32)
    for r in range(parts):
        for c in range(parts):
            s = (c - r) % parts
            if s <= parts // 2:
                idx_a[r, c], idx_s[r, c] = where(r), s
            else:
                idx_a[r, c], idx_s[r, c] = where(c), slots + (r - c) % parts
    blocks = both[idx_a, idx_s]
    return blocks.transpose(2, 0, 3, 1, 4).reshape(2, parts * rows, parts * rows)


def chip_ring(devices):
    chips = list(devices[0::2])
    coords = [tuple(d.coords) for d in chips]
    axes = [i for i in range(3) if len({c[i] for c in coords}) > 1]
    if len(axes) == 1:
        return sorted(range(len(chips)), key=lambda h: coords[h][axes[0]])
    if len(axes) == 2:
        slow, fast = axes if len({c[axes[1]] for c in coords}) == 2 else axes[::-1]
        if len({c[fast] for c in coords}) == 2:
            lo, hi = sorted({c[fast] for c in coords})
            first = sorted((h for h in range(len(chips)) if coords[h][fast] == lo), key=lambda h: coords[h][slow])
            second = sorted((h for h in range(len(chips)) if coords[h][fast] == hi), key=lambda h: -coords[h][slow])
            return first + second
    return list(range(len(chips)))


def ring_gather(mine, ring, here):
    chips = len(ring)
    parts = 2 * chips
    position = np.zeros(chips, np.int32)
    for k, h in enumerate(ring):
        position[h] = k
    order = jnp.asarray(np.array(ring, np.int32))
    core = here % 2
    pos = jnp.asarray(position)[here // 2]
    ahead = [(ring[k] * 2 + c, ring[(k + 1) % chips] * 2 + c) for k in range(chips) for c in range(2)]
    behind = [(b, a) for a, b in ahead]
    sibling = [(a, a ^ 1) for a in range(parts)]
    out = jnp.zeros((parts,) + mine.shape, mine.dtype)
    out = lax.dynamic_update_slice(out, mine[None], (here, 0, 0, 0, 0))
    out = lax.dynamic_update_slice(out, lax.ppermute(mine, AXES, sibling)[None], (here ^ 1, 0, 0, 0, 0))
    fwd, back = mine[:, 0], mine[:, 1]
    for t in range(1, chips):
        fwd = lax.ppermute(fwd, AXES, ahead)
        back = lax.ppermute(back, AXES, behind)
        src_fwd = order[(pos - t) % chips] * 2 + core
        src_back = order[(pos + t) % chips] * 2 + core
        out = lax.dynamic_update_slice(out, fwd[None, :, None], (src_fwd, 0, 0, 0, 0))
        out = lax.dynamic_update_slice(out, back[None, :, None], (src_back, 0, 1, 0, 0))
        out = lax.dynamic_update_slice(out, lax.ppermute(fwd, AXES, sibling)[None, :, None], (src_fwd ^ 1, 0, 0, 0, 0))
        out = lax.dynamic_update_slice(out, lax.ppermute(back, AXES, sibling)[None, :, None], (src_back ^ 1, 0, 1, 0, 0))
    return out


def assemble_kernel(*refs):
    pieces = len(refs) - 5
    g_refs, (re_ref, im_ref, upper, lower, sem) = refs[:pieces], refs[pieces:]
    parts = g_refs[0].shape[0]
    rows = g_refs[0].shape[-1]
    bounds = chunk_bounds(parts // 2 + 1, pieces)
    r = pl.program_id(0)

    def copies(row, slot):
        out = []
        for k, (lo, hi) in enumerate(bounds):
            out.append(pltpu.make_async_copy(g_refs[k].at[row], upper.at[slot, pl.ds(lo, hi - lo)], sem.at[slot, k]))
        for t in range(1, parts // 2):
            a = (row + parts - t) % parts
            k = [k for k, (lo, hi) in enumerate(bounds) if lo <= t < hi][0]
            src = g_refs[k].at[a, t - bounds[k][0]]
            out.append(pltpu.make_async_copy(src, lower.at[slot, t], sem.at[slot, pieces + t]))
        return out

    @pl.when(r == 0)
    def _():
        for copy in copies(r, 0):
            copy.start()

    @pl.when(r + 1 < parts)
    def _():
        for copy in copies(r + 1, (r + 1) % 2):
            copy.start()

    slot = r % 2
    for copy in copies(r, slot):
        copy.wait()
    for s in range(parts):
        col = pl.multiple_of(((r + s) % parts) * rows, rows)
        for k, out in ((0, re_ref), (1, im_ref)):
            if s <= parts // 2:
                block = upper[slot, s, k]
            else:
                block = lower[slot, parts - s, k].astype(jnp.float32).T.astype(jnp.bfloat16)
            out[:, pl.ds(col, rows)] = block


def assemble_pallas(chunks):
    parts = chunks[0].shape[0]
    rows = chunks[0].shape[-1]
    slots = sum(c.shape[1] for c in chunks)
    order = parts * rows
    return pl.pallas_call(
        assemble_kernel,
        grid=(parts,),
        in_specs=[pl.BlockSpec(memory_space=pl.ANY)] * len(chunks),
        out_specs=[pl.BlockSpec((rows, order), lambda r: (r, 0))] * 2,
        out_shape=[jax.ShapeDtypeStruct((order, order), jnp.bfloat16)] * 2,
        scratch_shapes=[
            pltpu.VMEM((2, slots, 2, rows, rows), jnp.bfloat16),
            pltpu.VMEM((2, parts // 2, 2, rows, rows), jnp.bfloat16),
            pltpu.SemaphoreType.DMA((2, len(chunks) + parts // 2)),
        ],
        compiler_params=pltpu.CompilerParams(dimension_semantics=("arbitrary",)),
    )(*chunks)


def local(data_field, primary_field, station_weight, adaptive_filter, ring=None):
    rows = data_field.shape[1]
    order = data_field.shape[2]
    chips = lax.axis_size("chip")
    cores = lax.axis_size("core")
    parts = chips * cores
    here = lax.axis_index("chip") * cores + lax.axis_index("core")
    mine = jnp.concatenate(upper_blocks(data_field, station_weight, parts, here), axis=0)
    if ring is not None and cores == 2 and len(ring) * 2 == parts:
        gathered = [ring_gather(mine, ring, here)]
    else:
        gathered = [lax.all_gather(mine, AXES)]
    if rows % 128 == 0:
        operator = assemble_pallas(gathered)
    else:
        operator = assemble(jnp.concatenate(gathered, axis=1)[None], parts, 1)
    factor = 0.8 / math.sqrt(order)
    current = primary_field
    prediction = jnp.zeros(data_field.shape, jnp.float32)
    for step in range(ORDERS):
        stacked = current.reshape(2 * rows, order)
        with_real = jnp.dot(stacked, operator[0], preferred_element_type=jnp.float32)
        with_imag = jnp.dot(stacked, operator[1], preferred_element_type=jnp.float32)
        real_part = (with_real[:rows] - with_imag[rows:]) * factor
        imag_part = (with_imag[:rows] + with_real[rows:]) * factor
        current = jnp.stack([real_part, imag_part]).astype(jnp.bfloat16)
        prediction = prediction + current.astype(jnp.float32)
    filt_re = adaptive_filter[0][None, :]
    filt_im = adaptive_filter[1][None, :]
    out_re = data_field[0].astype(jnp.float32) - (filt_re * prediction[0] - filt_im * prediction[1])
    out_im = data_field[1].astype(jnp.float32) - (filt_re * prediction[1] + filt_im * prediction[0])
    return jnp.stack([out_re, out_im])


def solution(mesh):
    groups, parts = mesh.devices.shape
    split = Mesh(mesh.devices.reshape(groups, parts // 2, 2), ("grp",) + AXES)
    rows_spec = P(None, ("grp",) + AXES, None)
    try:
        ring = chip_ring(list(mesh.devices[0]))
    except (AttributeError, TypeError):
        ring = None
    return jax.shard_map(
        functools.partial(local, ring=ring),
        mesh=split,
        in_specs=(rows_spec, rows_spec, P(), P(None, "grp")),
        out_specs=rows_spec,
        check_vma=False,
    )
```

```python
import functools
import math

import numpy as np
import jax
import jax.numpy as jnp
from jax import lax
from jax.experimental import pallas as pl
from jax.experimental.pallas import tpu as pltpu
from jax.sharding import Mesh, PartitionSpec as P

ORDERS = 12
AXES = ("chip", "core")


def blend_rows(field, mirror, left_weight, right_weight):
    top = left_weight[:, None] * field.astype(jnp.float32) + right_weight[None, :] * mirror.astype(
        jnp.float32
    )
    return (top / (left_weight[:, None] + right_weight[None, :])).astype(jnp.bfloat16)


def upper_blocks(data_field, station_weight, parts, here):
    rows = data_field.shape[1]
    half = parts // 2
    rolled = jnp.roll(data_field.reshape(2, rows, parts, rows), -here, axis=2)
    own = rolled[:, :, : half + 1]
    received = [rolled[:, :, 0]]
    for s in range(1, half + 1):
        perm = [(c, (c - s) % parts) for c in range(parts)]
        received.append(lax.ppermute(rolled[:, :, parts - s], AXES, perm=perm))
    own_weight = lax.dynamic_slice_in_dim(station_weight, here * rows, rows)[:, None, None]
    col_weight = jnp.roll(station_weight.reshape(parts, rows), -here, axis=0)[None, : half + 1]
    chunks = []
    for lo, hi in chunk_bounds(half + 1):
        mirror = jnp.stack(received[lo:hi], axis=2).transpose(0, 3, 2, 1)
        top = own_weight * own[:, :, lo:hi].astype(jnp.float32) + col_weight[:, lo:hi] * mirror.astype(jnp.float32)
        blended = (top / (own_weight + col_weight[:, lo:hi])).astype(jnp.bfloat16)
        chunks.append(blended.transpose(2, 0, 1, 3))
    return chunks


def chunk_bounds(slots, pieces=3):
    edges = [round(i * slots / pieces) for i in range(pieces + 1)]
    return list(zip(edges[:-1], edges[1:]))


def assemble(gathered, chips, cores):
    parts = chips * cores
    slots = gathered.shape[2]
    rows = gathered.shape[-1]
    flat = gathered.reshape((parts, slots) + gathered.shape[3:])
    both = jnp.concatenate([flat, flat.swapaxes(-1, -2)], axis=1)
    where = lambda a: (a % cores) * chips + a // cores
    idx_a = np.zeros((parts, parts), np.int32)
    idx_s = np.zeros((parts, parts), np.int32)
    for r in range(parts):
        for c in range(parts):
            s = (c - r) % parts
            if s <= parts // 2:
                idx_a[r, c], idx_s[r, c] = where(r), s
            else:
                idx_a[r, c], idx_s[r, c] = where(c), slots + (r - c) % parts
    blocks = both[idx_a, idx_s]
    return blocks.transpose(2, 0, 3, 1, 4).reshape(2, parts * rows, parts * rows)


def chip_ring(devices):
    chips = list(devices[0::2])
    coords = [tuple(d.coords) for d in chips]
    axes = [i for i in range(3) if len({c[i] for c in coords}) > 1]
    if len(axes) == 1:
        return sorted(range(len(chips)), key=lambda h: coords[h][axes[0]])
    if len(axes) == 2:
        slow, fast = axes if len({c[axes[1]] for c in coords}) == 2 else axes[::-1]
        if len({c[fast] for c in coords}) == 2:
            lo, hi = sorted({c[fast] for c in coords})
            first = sorted((h for h in range(len(chips)) if coords[h][fast] == lo), key=lambda h: coords[h][slow])
            second = sorted((h for h in range(len(chips)) if coords[h][fast] == hi), key=lambda h: -coords[h][slow])
            return first + second
    return list(range(len(chips)))


def ring_gather(mine, ring, here):
    chips = len(ring)
    parts = 2 * chips
    core = here % 2
    chip = here // 2

    def ring_source(t):
        pick = 0
        for k, h in enumerate(ring):
            pick = pick + jnp.where(chip == h, ring[(k - t) % chips], 0)
        return pick

    ahead = [(ring[k] * 2 + c, ring[(k + 1) % chips] * 2 + c) for k in range(chips) for c in range(2)]
    behind = [(b, a) for a, b in ahead]
    sibling = [(a, a ^ 1) for a in range(parts)]
    out = jnp.zeros((parts,) + mine.shape, mine.dtype)
    out = lax.dynamic_update_slice(out, mine[None], (here, 0, 0, 0, 0))
    out = lax.dynamic_update_slice(out, lax.ppermute(mine, AXES, sibling)[None], (here ^ 1, 0, 0, 0, 0))
    fwd, back = mine[:, 0], mine[:, 1]
    for t in range(1, chips):
        fwd = lax.ppermute(fwd, AXES, ahead)
        back = lax.ppermute(back, AXES, behind)
        src_fwd = ring_source(t) * 2 + core
        src_back = ring_source(-t) * 2 + core
        out = lax.dynamic_update_slice(out, fwd[None, :, None], (src_fwd, 0, 0, 0, 0))
        out = lax.dynamic_update_slice(out, back[None, :, None], (src_back, 0, 1, 0, 0))
        out = lax.dynamic_update_slice(out, lax.ppermute(fwd, AXES, sibling)[None, :, None], (src_fwd ^ 1, 0, 0, 0, 0))
        out = lax.dynamic_update_slice(out, lax.ppermute(back, AXES, sibling)[None, :, None], (src_back ^ 1, 0, 1, 0, 0))
    return out


def assemble_kernel(*refs):
    pieces = len(refs) - 5
    g_refs, (re_ref, im_ref, upper, lower, sem) = refs[:pieces], refs[pieces:]
    parts = g_refs[0].shape[0]
    rows = g_refs[0].shape[-1]
    bounds = chunk_bounds(parts // 2 + 1, pieces)
    r = pl.program_id(0)

    def copies(row, slot):
        out = []
        for k, (lo, hi) in enumerate(bounds):
            out.append(pltpu.make_async_copy(g_refs[k].at[row], upper.at[slot, pl.ds(lo, hi - lo)], sem.at[slot, k]))
        for t in range(1, parts // 2):
            a = (row + parts - t) % parts
            k = [k for k, (lo, hi) in enumerate(bounds) if lo <= t < hi][0]
            src = g_refs[k].at[a, t - bounds[k][0]]
            out.append(pltpu.make_async_copy(src, lower.at[slot, t], sem.at[slot, pieces + t]))
        return out

    @pl.when(r == 0)
    def _():
        for copy in copies(r, 0):
            copy.start()

    @pl.when(r + 1 < parts)
    def _():
        for copy in copies(r + 1, (r + 1) % 2):
            copy.start()

    slot = r % 2
    for copy in copies(r, slot):
        copy.wait()
    for s in range(parts):
        col = pl.multiple_of(((r + s) % parts) * rows, rows)
        for k, out in ((0, re_ref), (1, im_ref)):
            if s <= parts // 2:
                block = upper[slot, s, k]
            else:
                block = lower[slot, parts - s, k].astype(jnp.float32).T.astype(jnp.bfloat16)
            out[:, pl.ds(col, rows)] = block


def assemble_pallas(chunks):
    parts = chunks[0].shape[0]
    rows = chunks[0].shape[-1]
    slots = sum(c.shape[1] for c in chunks)
    order = parts * rows
    return pl.pallas_call(
        assemble_kernel,
        grid=(parts,),
        in_specs=[pl.BlockSpec(memory_space=pl.ANY)] * len(chunks),
        out_specs=[pl.BlockSpec((rows, order), lambda r: (r, 0))] * 2,
        out_shape=[jax.ShapeDtypeStruct((order, order), jnp.bfloat16)] * 2,
        scratch_shapes=[
            pltpu.VMEM((2, slots, 2, rows, rows), jnp.bfloat16),
            pltpu.VMEM((2, parts // 2, 2, rows, rows), jnp.bfloat16),
            pltpu.SemaphoreType.DMA((2, len(chunks) + parts // 2)),
        ],
        compiler_params=pltpu.CompilerParams(dimension_semantics=("arbitrary",)),
    )(*chunks)


def local(data_field, primary_field, station_weight, adaptive_filter, ring=None):
    rows = data_field.shape[1]
    order = data_field.shape[2]
    chips = lax.axis_size("chip")
    cores = lax.axis_size("core")
    parts = chips * cores
    here = lax.axis_index("chip") * cores + lax.axis_index("core")
    mine = jnp.concatenate(upper_blocks(data_field, station_weight, parts, here), axis=0)
    if ring is not None and cores == 2 and len(ring) * 2 == parts:
        gathered = [ring_gather(mine, ring, here)]
    else:
        gathered = [lax.all_gather(mine, AXES)]
    if rows % 128 == 0:
        operator = assemble_pallas(gathered)
    else:
        operator = assemble(jnp.concatenate(gathered, axis=1)[None], parts, 1)
    factor = 0.8 / math.sqrt(order)
    current = primary_field
    prediction = jnp.zeros(data_field.shape, jnp.float32)
    for step in range(ORDERS):
        stacked = current.reshape(2 * rows, order)
        with_real = jnp.dot(stacked, operator[0], preferred_element_type=jnp.float32)
        with_imag = jnp.dot(stacked, operator[1], preferred_element_type=jnp.float32)
        real_part = (with_real[:rows] - with_imag[rows:]) * factor
        imag_part = (with_imag[:rows] + with_real[rows:]) * factor
        current = jnp.stack([real_part, imag_part]).astype(jnp.bfloat16)
        prediction = prediction + current.astype(jnp.float32)
    filt_re = adaptive_filter[0][None, :]
    filt_im = adaptive_filter[1][None, :]
    out_re = data_field[0].astype(jnp.float32) - (filt_re * prediction[0] - filt_im * prediction[1])
    out_im = data_field[1].astype(jnp.float32) - (filt_re * prediction[1] + filt_im * prediction[0])
    return jnp.stack([out_re, out_im])


def solution(mesh):
    groups, parts = mesh.devices.shape
    split = Mesh(mesh.devices.reshape(groups, parts // 2, 2), ("grp",) + AXES)
    rows_spec = P(None, ("grp",) + AXES, None)
    try:
        ring = chip_ring(list(mesh.devices[0]))
    except (AttributeError, TypeError):
        ring = None
    return jax.shard_map(
        functools.partial(local, ring=ring),
        mesh=split,
        in_specs=(rows_spec, rows_spec, P(), P(None, "grp")),
        out_specs=rows_spec,
        check_vma=False,
    )
```

```python
import functools
import math

import numpy as np
import jax
import jax.numpy as jnp
from jax import lax
from jax.experimental import pallas as pl
from jax.experimental.pallas import tpu as pltpu
from jax.sharding import Mesh, PartitionSpec as P

ORDERS = 12
AXES = ("chip", "core")


def blend_rows(field, mirror, left_weight, right_weight):
    top = left_weight[:, None] * field.astype(jnp.float32) + right_weight[None, :] * mirror.astype(
        jnp.float32
    )
    return (top / (left_weight[:, None] + right_weight[None, :])).astype(jnp.bfloat16)


def upper_blocks(data_field, station_weight, parts, here):
    rows = data_field.shape[1]
    half = parts // 2
    rolled = jnp.roll(data_field.reshape(2, rows, parts, rows), -here, axis=2)
    own = rolled[:, :, : half + 1]
    received = [rolled[:, :, 0]]
    for s in range(1, half + 1):
        perm = [(c, (c - s) % parts) for c in range(parts)]
        received.append(lax.ppermute(rolled[:, :, parts - s], AXES, perm=perm))
    own_weight = lax.dynamic_slice_in_dim(station_weight, here * rows, rows)[:, None, None]
    col_weight = jnp.roll(station_weight.reshape(parts, rows), -here, axis=0)[None, : half + 1]
    chunks = []
    for lo, hi in chunk_bounds(half + 1):
        mirror = jnp.stack(received[lo:hi], axis=2).transpose(0, 3, 2, 1)
        top = own_weight * own[:, :, lo:hi].astype(jnp.float32) + col_weight[:, lo:hi] * mirror.astype(jnp.float32)
        blended = (top / (own_weight + col_weight[:, lo:hi])).astype(jnp.bfloat16)
        chunks.append(blended.transpose(2, 0, 1, 3))
    return chunks


def chunk_bounds(slots, pieces=3):
    edges = [round(i * slots / pieces) for i in range(pieces + 1)]
    return list(zip(edges[:-1], edges[1:]))


def assemble(gathered, chips, cores):
    parts = chips * cores
    slots = gathered.shape[2]
    rows = gathered.shape[-1]
    flat = gathered.reshape((parts, slots) + gathered.shape[3:])
    both = jnp.concatenate([flat, flat.swapaxes(-1, -2)], axis=1)
    where = lambda a: (a % cores) * chips + a // cores
    idx_a = np.zeros((parts, parts), np.int32)
    idx_s = np.zeros((parts, parts), np.int32)
    for r in range(parts):
        for c in range(parts):
            s = (c - r) % parts
            if s <= parts // 2:
                idx_a[r, c], idx_s[r, c] = where(r), s
            else:
                idx_a[r, c], idx_s[r, c] = where(c), slots + (r - c) % parts
    blocks = both[idx_a, idx_s]
    return blocks.transpose(2, 0, 3, 1, 4).reshape(2, parts * rows, parts * rows)


def chip_ring(devices):
    chips = list(devices[0::2])
    coords = [tuple(d.coords) for d in chips]
    axes = [i for i in range(3) if len({c[i] for c in coords}) > 1]
    if len(axes) == 1:
        return sorted(range(len(chips)), key=lambda h: coords[h][axes[0]])
    if len(axes) == 2:
        slow, fast = axes if len({c[axes[1]] for c in coords}) == 2 else axes[::-1]
        if len({c[fast] for c in coords}) == 2:
            lo, hi = sorted({c[fast] for c in coords})
            first = sorted((h for h in range(len(chips)) if coords[h][fast] == lo), key=lambda h: coords[h][slow])
            second = sorted((h for h in range(len(chips)) if coords[h][fast] == hi), key=lambda h: -coords[h][slow])
            return first + second
    return list(range(len(chips)))


def ring_gather(mine, ring, here):
    chips = len(ring)
    parts = 2 * chips
    core = here % 2
    chip = here // 2

    def ring_source(t):
        pick = 0
        for k, h in enumerate(ring):
            pick = pick + jnp.where(chip == h, ring[(k - t) % chips], 0)
        return pick

    ahead = [(ring[k] * 2 + c, ring[(k + 1) % chips] * 2 + c) for k in range(chips) for c in range(2)]
    behind = [(b, a) for a, b in ahead]
    sibling = [(a, a ^ 1) for a in range(parts)]
    out = pl.pallas_call(
        lambda ref: None,
        out_shape=jax.ShapeDtypeStruct((parts,) + mine.shape, mine.dtype),
        out_specs=pl.BlockSpec(memory_space=pl.ANY),
    )()
    out = lax.dynamic_update_slice(out, mine[None], (here, 0, 0, 0, 0))
    out = lax.dynamic_update_slice(out, lax.ppermute(mine, AXES, sibling)[None], (here ^ 1, 0, 0, 0, 0))
    fwd, back = mine[:, 0], mine[:, 1]
    for t in range(1, chips):
        fwd = lax.ppermute(fwd, AXES, ahead)
        back = lax.ppermute(back, AXES, behind)
        src_fwd = ring_source(t) * 2 + core
        src_back = ring_source(-t) * 2 + core
        out = lax.dynamic_update_slice(out, fwd[None, :, None], (src_fwd, 0, 0, 0, 0))
        out = lax.dynamic_update_slice(out, back[None, :, None], (src_back, 0, 1, 0, 0))
        out = lax.dynamic_update_slice(out, lax.ppermute(fwd, AXES, sibling)[None, :, None], (src_fwd ^ 1, 0, 0, 0, 0))
        out = lax.dynamic_update_slice(out, lax.ppermute(back, AXES, sibling)[None, :, None], (src_back ^ 1, 0, 1, 0, 0))
    return out


def assemble_kernel(*refs):
    pieces = len(refs) - 5
    g_refs, (re_ref, im_ref, upper, lower, sem) = refs[:pieces], refs[pieces:]
    parts = g_refs[0].shape[0]
    rows = g_refs[0].shape[-1]
    bounds = chunk_bounds(parts // 2 + 1, pieces)
    r = pl.program_id(0)

    def copies(row, slot):
        out = []
        for k, (lo, hi) in enumerate(bounds):
            out.append(pltpu.make_async_copy(g_refs[k].at[row], upper.at[slot, pl.ds(lo, hi - lo)], sem.at[slot, k]))
        for t in range(1, parts // 2):
            a = (row + parts - t) % parts
            k = [k for k, (lo, hi) in enumerate(bounds) if lo <= t < hi][0]
            src = g_refs[k].at[a, t - bounds[k][0]]
            out.append(pltpu.make_async_copy(src, lower.at[slot, t], sem.at[slot, pieces + t]))
        return out

    @pl.when(r == 0)
    def _():
        for copy in copies(r, 0):
            copy.start()

    @pl.when(r + 1 < parts)
    def _():
        for copy in copies(r + 1, (r + 1) % 2):
            copy.start()

    slot = r % 2
    for copy in copies(r, slot):
        copy.wait()
    for s in range(parts):
        col = pl.multiple_of(((r + s) % parts) * rows, rows)
        for k, out in ((0, re_ref), (1, im_ref)):
            if s <= parts // 2:
                block = upper[slot, s, k]
            else:
                block = lower[slot, parts - s, k].astype(jnp.float32).T.astype(jnp.bfloat16)
            out[:, pl.ds(col, rows)] = block


def assemble_pallas(chunks):
    parts = chunks[0].shape[0]
    rows = chunks[0].shape[-1]
    slots = sum(c.shape[1] for c in chunks)
    order = parts * rows
    return pl.pallas_call(
        assemble_kernel,
        grid=(parts,),
        in_specs=[pl.BlockSpec(memory_space=pl.ANY)] * len(chunks),
        out_specs=[pl.BlockSpec((rows, order), lambda r: (r, 0))] * 2,
        out_shape=[jax.ShapeDtypeStruct((order, order), jnp.bfloat16)] * 2,
        scratch_shapes=[
            pltpu.VMEM((2, slots, 2, rows, rows), jnp.bfloat16),
            pltpu.VMEM((2, parts // 2, 2, rows, rows), jnp.bfloat16),
            pltpu.SemaphoreType.DMA((2, len(chunks) + parts // 2)),
        ],
        compiler_params=pltpu.CompilerParams(dimension_semantics=("arbitrary",)),
    )(*chunks)


def local(data_field, primary_field, station_weight, adaptive_filter, ring=None):
    rows = data_field.shape[1]
    order = data_field.shape[2]
    chips = lax.axis_size("chip")
    cores = lax.axis_size("core")
    parts = chips * cores
    here = lax.axis_index("chip") * cores + lax.axis_index("core")
    mine = jnp.concatenate(upper_blocks(data_field, station_weight, parts, here), axis=0)
    if ring is not None and cores == 2 and len(ring) * 2 == parts:
        gathered = [ring_gather(mine, ring, here)]
    else:
        gathered = [lax.all_gather(mine, AXES)]
    if rows % 128 == 0:
        operator = assemble_pallas(gathered)
    else:
        operator = assemble(jnp.concatenate(gathered, axis=1)[None], parts, 1)
    factor = 0.8 / math.sqrt(order)
    current = primary_field
    prediction = jnp.zeros(data_field.shape, jnp.float32)
    for step in range(ORDERS):
        stacked = current.reshape(2 * rows, order)
        with_real = jnp.dot(stacked, operator[0], preferred_element_type=jnp.float32)
        with_imag = jnp.dot(stacked, operator[1], preferred_element_type=jnp.float32)
        real_part = (with_real[:rows] - with_imag[rows:]) * factor
        imag_part = (with_imag[:rows] + with_real[rows:]) * factor
        current = jnp.stack([real_part, imag_part]).astype(jnp.bfloat16)
        prediction = prediction + current.astype(jnp.float32)
    filt_re = adaptive_filter[0][None, :]
    filt_im = adaptive_filter[1][None, :]
    out_re = data_field[0].astype(jnp.float32) - (filt_re * prediction[0] - filt_im * prediction[1])
    out_im = data_field[1].astype(jnp.float32) - (filt_re * prediction[1] + filt_im * prediction[0])
    return jnp.stack([out_re, out_im])


def solution(mesh):
    groups, parts = mesh.devices.shape
    split = Mesh(mesh.devices.reshape(groups, parts // 2, 2), ("grp",) + AXES)
    rows_spec = P(None, ("grp",) + AXES, None)
    try:
        ring = chip_ring(list(mesh.devices[0]))
    except (AttributeError, TypeError):
        ring = None
    return jax.shard_map(
        functools.partial(local, ring=ring),
        mesh=split,
        in_specs=(rows_spec, rows_spec, P(), P(None, "grp")),
        out_specs=rows_spec,
        check_vma=False,
    )
```

```python
import functools
import math

import numpy as np
import jax
import jax.numpy as jnp
from jax import lax
from jax.experimental import pallas as pl
from jax.experimental.pallas import tpu as pltpu
from jax.sharding import Mesh, PartitionSpec as P

ORDERS = 12
AXES = ("chip", "core")


def blend_rows(field, mirror, left_weight, right_weight):
    top = left_weight[:, None] * field.astype(jnp.float32) + right_weight[None, :] * mirror.astype(
        jnp.float32
    )
    return (top / (left_weight[:, None] + right_weight[None, :])).astype(jnp.bfloat16)


def upper_blocks(data_field, station_weight, parts, here):
    rows = data_field.shape[1]
    half = parts // 2
    rolled = jnp.roll(data_field.reshape(2, rows, parts, rows), -here, axis=2)
    own = rolled[:, :, : half + 1]
    received = [rolled[:, :, 0]]
    for s in range(1, half + 1):
        perm = [(c, (c - s) % parts) for c in range(parts)]
        received.append(lax.ppermute(rolled[:, :, parts - s], AXES, perm=perm))
    own_weight = lax.dynamic_slice_in_dim(station_weight, here * rows, rows)[:, None, None]
    col_weight = jnp.roll(station_weight.reshape(parts, rows), -here, axis=0)[None, : half + 1]
    chunks = []
    for lo, hi in chunk_bounds(half + 1):
        mirror = jnp.stack(received[lo:hi], axis=2).transpose(0, 3, 2, 1)
        top = own_weight * own[:, :, lo:hi].astype(jnp.float32) + col_weight[:, lo:hi] * mirror.astype(jnp.float32)
        blended = (top / (own_weight + col_weight[:, lo:hi])).astype(jnp.bfloat16)
        chunks.append(blended.transpose(2, 0, 1, 3))
    return chunks


def chunk_bounds(slots, pieces=3):
    edges = [round(i * slots / pieces) for i in range(pieces + 1)]
    return list(zip(edges[:-1], edges[1:]))


def assemble(gathered, chips, cores):
    parts = chips * cores
    slots = gathered.shape[2]
    rows = gathered.shape[-1]
    flat = gathered.reshape((parts, slots) + gathered.shape[3:])
    both = jnp.concatenate([flat, flat.swapaxes(-1, -2)], axis=1)
    where = lambda a: (a % cores) * chips + a // cores
    idx_a = np.zeros((parts, parts), np.int32)
    idx_s = np.zeros((parts, parts), np.int32)
    for r in range(parts):
        for c in range(parts):
            s = (c - r) % parts
            if s <= parts // 2:
                idx_a[r, c], idx_s[r, c] = where(r), s
            else:
                idx_a[r, c], idx_s[r, c] = where(c), slots + (r - c) % parts
    blocks = both[idx_a, idx_s]
    return blocks.transpose(2, 0, 3, 1, 4).reshape(2, parts * rows, parts * rows)


def chip_ring(devices):
    chips = list(devices[0::2])
    coords = [tuple(d.coords) for d in chips]
    axes = [i for i in range(3) if len({c[i] for c in coords}) > 1]
    if len(axes) == 1:
        return sorted(range(len(chips)), key=lambda h: coords[h][axes[0]])
    if len(axes) == 2:
        slow, fast = axes if len({c[axes[1]] for c in coords}) == 2 else axes[::-1]
        if len({c[fast] for c in coords}) == 2:
            lo, hi = sorted({c[fast] for c in coords})
            first = sorted((h for h in range(len(chips)) if coords[h][fast] == lo), key=lambda h: coords[h][slow])
            second = sorted((h for h in range(len(chips)) if coords[h][fast] == hi), key=lambda h: -coords[h][slow])
            return first + second
    return list(range(len(chips)))


def ring_gather(mine, ring, here):
    chips = len(ring)
    parts = 2 * chips
    core = here % 2
    chip = here // 2

    def ring_source(t):
        pick = 0
        for k, h in enumerate(ring):
            pick = pick + jnp.where(chip == h, ring[(k - t) % chips], 0)
        return pick

    ahead = [(ring[k] * 2 + c, ring[(k + 1) % chips] * 2 + c) for k in range(chips) for c in range(2)]
    behind = [(b, a) for a, b in ahead]
    sibling = [(a, a ^ 1) for a in range(parts)]
    out = pl.pallas_call(
        lambda ref: None,
        out_shape=jax.ShapeDtypeStruct((parts,) + mine.shape, mine.dtype),
        out_specs=pl.BlockSpec(memory_space=pl.ANY),
    )()
    out = lax.dynamic_update_slice(out, mine[None], (here, 0, 0, 0, 0))
    out = lax.dynamic_update_slice(out, lax.ppermute(mine, AXES, sibling)[None], (here ^ 1, 0, 0, 0, 0))
    fwd, back = mine[:, 0], mine[:, 1]
    for t in range(1, chips):
        fwd = lax.ppermute(fwd, AXES, ahead)
        back = lax.ppermute(back, AXES, behind)
        src_fwd = ring_source(t) * 2 + core
        src_back = ring_source(-t) * 2 + core
        out = lax.dynamic_update_slice(out, fwd[None, :, None], (src_fwd, 0, 0, 0, 0))
        out = lax.dynamic_update_slice(out, back[None, :, None], (src_back, 0, 1, 0, 0))
        out = lax.dynamic_update_slice(out, lax.ppermute(fwd, AXES, sibling)[None, :, None], (src_fwd ^ 1, 0, 0, 0, 0))
        out = lax.dynamic_update_slice(out, lax.ppermute(back, AXES, sibling)[None, :, None], (src_back ^ 1, 0, 1, 0, 0))
    return out


def assemble_kernel(*refs):
    pieces = len(refs) - 5
    g_refs, (re_ref, im_ref, upper, lower, sem) = refs[:pieces], refs[pieces:]
    parts = g_refs[0].shape[0]
    rows = g_refs[0].shape[-1]
    bounds = chunk_bounds(parts // 2 + 1, pieces)
    r = pl.program_id(0)

    def copies(row, slot):
        out = []
        for k, (lo, hi) in enumerate(bounds):
            out.append(pltpu.make_async_copy(g_refs[k].at[row], upper.at[slot, pl.ds(lo, hi - lo)], sem.at[slot, k]))
        for t in range(1, parts // 2):
            a = (row + parts - t) % parts
            k = [k for k, (lo, hi) in enumerate(bounds) if lo <= t < hi][0]
            src = g_refs[k].at[a, t - bounds[k][0]]
            out.append(pltpu.make_async_copy(src, lower.at[slot, t], sem.at[slot, pieces + t]))
        return out

    @pl.when(r == 0)
    def _():
        for copy in copies(r, 0):
            copy.start()

    @pl.when(r + 1 < parts)
    def _():
        for copy in copies(r + 1, (r + 1) % 2):
            copy.start()

    slot = r % 2
    for copy in copies(r, slot):
        copy.wait()
    for s in range(parts):
        col = pl.multiple_of(((r + s) % parts) * rows, rows)
        for k, out in ((0, re_ref), (1, im_ref)):
            if s <= parts // 2:
                block = upper[slot, s, k]
            else:
                block = lower[slot, parts - s, k].T
            out[:, pl.ds(col, rows)] = block


def assemble_pallas(chunks):
    parts = chunks[0].shape[0]
    rows = chunks[0].shape[-1]
    slots = sum(c.shape[1] for c in chunks)
    order = parts * rows
    return pl.pallas_call(
        assemble_kernel,
        grid=(parts,),
        in_specs=[pl.BlockSpec(memory_space=pl.ANY)] * len(chunks),
        out_specs=[pl.BlockSpec((rows, order), lambda r: (r, 0))] * 2,
        out_shape=[jax.ShapeDtypeStruct((order, order), jnp.bfloat16)] * 2,
        scratch_shapes=[
            pltpu.VMEM((2, slots, 2, rows, rows), jnp.bfloat16),
            pltpu.VMEM((2, parts // 2, 2, rows, rows), jnp.bfloat16),
            pltpu.SemaphoreType.DMA((2, len(chunks) + parts // 2)),
        ],
        compiler_params=pltpu.CompilerParams(dimension_semantics=("arbitrary",)),
    )(*chunks)


def local(data_field, primary_field, station_weight, adaptive_filter, ring=None):
    rows = data_field.shape[1]
    order = data_field.shape[2]
    chips = lax.axis_size("chip")
    cores = lax.axis_size("core")
    parts = chips * cores
    here = lax.axis_index("chip") * cores + lax.axis_index("core")
    mine = jnp.concatenate(upper_blocks(data_field, station_weight, parts, here), axis=0)
    if ring is not None and cores == 2 and len(ring) * 2 == parts:
        gathered = [ring_gather(mine, ring, here)]
    else:
        gathered = [lax.all_gather(mine, AXES)]
    if rows % 128 == 0:
        operator = assemble_pallas(gathered)
    else:
        operator = assemble(jnp.concatenate(gathered, axis=1)[None], parts, 1)
    factor = 0.8 / math.sqrt(order)
    current = primary_field
    prediction = jnp.zeros(data_field.shape, jnp.float32)
    for step in range(ORDERS):
        stacked = current.reshape(2 * rows, order)
        with_real = jnp.dot(stacked, operator[0], preferred_element_type=jnp.float32)
        with_imag = jnp.dot(stacked, operator[1], preferred_element_type=jnp.float32)
        real_part = (with_real[:rows] - with_imag[rows:]) * factor
        imag_part = (with_imag[:rows] + with_real[rows:]) * factor
        current = jnp.stack([real_part, imag_part]).astype(jnp.bfloat16)
        prediction = prediction + current.astype(jnp.float32)
    filt_re = adaptive_filter[0][None, :]
    filt_im = adaptive_filter[1][None, :]
    out_re = data_field[0].astype(jnp.float32) - (filt_re * prediction[0] - filt_im * prediction[1])
    out_im = data_field[1].astype(jnp.float32) - (filt_re * prediction[1] + filt_im * prediction[0])
    return jnp.stack([out_re, out_im])


def solution(mesh):
    groups, parts = mesh.devices.shape
    split = Mesh(mesh.devices.reshape(groups, parts // 2, 2), ("grp",) + AXES)
    rows_spec = P(None, ("grp",) + AXES, None)
    try:
        ring = chip_ring(list(mesh.devices[0]))
    except (AttributeError, TypeError):
        ring = None
    return jax.shard_map(
        functools.partial(local, ring=ring),
        mesh=split,
        in_specs=(rows_spec, rows_spec, P(), P(None, "grp")),
        out_specs=rows_spec,
        check_vma=False,
    )
```

```python
import functools
import math

import numpy as np
import jax
import jax.numpy as jnp
from jax import lax
from jax.experimental import pallas as pl
from jax.experimental.pallas import tpu as pltpu
from jax.sharding import Mesh, PartitionSpec as P

ORDERS = 12
AXES = ("chip", "core")


def blend_rows(field, mirror, left_weight, right_weight):
    top = left_weight[:, None] * field.astype(jnp.float32) + right_weight[None, :] * mirror.astype(
        jnp.float32
    )
    return (top / (left_weight[:, None] + right_weight[None, :])).astype(jnp.bfloat16)


def upper_blocks(data_field, station_weight, parts, here):
    rows = data_field.shape[1]
    half = parts // 2
    rolled = jnp.roll(data_field.reshape(2, rows, parts, rows), -here, axis=2)
    own = rolled[:, :, : half + 1]
    received = [rolled[:, :, 0]]
    for s in range(1, half + 1):
        perm = [(c, (c - s) % parts) for c in range(parts)]
        received.append(lax.ppermute(rolled[:, :, parts - s], AXES, perm=perm))
    own_weight = lax.dynamic_slice_in_dim(station_weight, here * rows, rows)[:, None, None]
    col_weight = jnp.roll(station_weight.reshape(parts, rows), -here, axis=0)[None, : half + 1]
    chunks = []
    for lo, hi in chunk_bounds(half + 1):
        mirror = jnp.stack(received[lo:hi], axis=2).transpose(0, 3, 2, 1)
        top = own_weight * own[:, :, lo:hi].astype(jnp.float32) + col_weight[:, lo:hi] * mirror.astype(jnp.float32)
        blended = (top / (own_weight + col_weight[:, lo:hi])).astype(jnp.bfloat16)
        chunks.append(blended.transpose(2, 0, 1, 3))
    return chunks


def chunk_bounds(slots, pieces=3):
    edges = [round(i * slots / pieces) for i in range(pieces + 1)]
    return list(zip(edges[:-1], edges[1:]))


def assemble(gathered, chips, cores):
    parts = chips * cores
    slots = gathered.shape[2]
    rows = gathered.shape[-1]
    flat = gathered.reshape((parts, slots) + gathered.shape[3:])
    both = jnp.concatenate([flat, flat.swapaxes(-1, -2)], axis=1)
    where = lambda a: (a % cores) * chips + a // cores
    idx_a = np.zeros((parts, parts), np.int32)
    idx_s = np.zeros((parts, parts), np.int32)
    for r in range(parts):
        for c in range(parts):
            s = (c - r) % parts
            if s <= parts // 2:
                idx_a[r, c], idx_s[r, c] = where(r), s
            else:
                idx_a[r, c], idx_s[r, c] = where(c), slots + (r - c) % parts
    blocks = both[idx_a, idx_s]
    return blocks.transpose(2, 0, 3, 1, 4).reshape(2, parts * rows, parts * rows)


def chip_ring(devices):
    chips = list(devices[0::2])
    coords = [tuple(d.coords) for d in chips]
    axes = [i for i in range(3) if len({c[i] for c in coords}) > 1]
    if len(axes) == 1:
        return sorted(range(len(chips)), key=lambda h: coords[h][axes[0]])
    if len(axes) == 2:
        slow, fast = axes if len({c[axes[1]] for c in coords}) == 2 else axes[::-1]
        if len({c[fast] for c in coords}) == 2:
            lo, hi = sorted({c[fast] for c in coords})
            first = sorted((h for h in range(len(chips)) if coords[h][fast] == lo), key=lambda h: coords[h][slow])
            second = sorted((h for h in range(len(chips)) if coords[h][fast] == hi), key=lambda h: -coords[h][slow])
            return first + second
    return list(range(len(chips)))


def ring_gather(mine, ring, here):
    chips = len(ring)
    parts = 2 * chips
    core = here % 2
    chip = here // 2

    def ring_source(t):
        pick = 0
        for k, h in enumerate(ring):
            pick = pick + jnp.where(chip == h, ring[(k - t) % chips], 0)
        return pick

    ahead = [(ring[k] * 2 + c, ring[(k + 1) % chips] * 2 + c) for k in range(chips) for c in range(2)]
    behind = [(b, a) for a, b in ahead]
    sibling = [(a, a ^ 1) for a in range(parts)]
    out = pl.pallas_call(
        lambda ref: None,
        out_shape=jax.ShapeDtypeStruct((parts,) + mine.shape, mine.dtype),
        out_specs=pl.BlockSpec(memory_space=pl.ANY),
    )()
    out = lax.dynamic_update_slice(out, mine[None], (here, 0, 0, 0, 0))
    out = lax.dynamic_update_slice(out, lax.ppermute(mine, AXES, sibling)[None], (here ^ 1, 0, 0, 0, 0))
    fwd, back = mine[:, 0], mine[:, 1]
    for t in range(1, chips):
        fwd = lax.ppermute(fwd, AXES, ahead)
        back = lax.ppermute(back, AXES, behind)
        src_fwd = ring_source(t) * 2 + core
        src_back = ring_source(-t) * 2 + core
        out = lax.dynamic_update_slice(out, fwd[None, :, None], (src_fwd, 0, 0, 0, 0))
        out = lax.dynamic_update_slice(out, back[None, :, None], (src_back, 0, 1, 0, 0))
        out = lax.dynamic_update_slice(out, lax.ppermute(fwd, AXES, sibling)[None, :, None], (src_fwd ^ 1, 0, 0, 0, 0))
        out = lax.dynamic_update_slice(out, lax.ppermute(back, AXES, sibling)[None, :, None], (src_back ^ 1, 0, 1, 0, 0))
    return out


def assemble_kernel(*refs):
    g_ref, re_ref, im_ref, lower, flipped, sem_in, sem_up, sem_lo = refs
    parts, slots = g_ref.shape[:2]
    rows = g_ref.shape[-1]
    outs = (re_ref, im_ref)
    r = pl.program_id(0)

    def fetches(row, slot):
        out = []
        for t in range(1, parts // 2):
            src = g_ref.at[(row + parts - t) % parts, t]
            out.append(pltpu.make_async_copy(src, lower.at[slot, t], sem_in.at[slot, t]))
        return out

    @pl.when(r == 0)
    def _():
        for copy in fetches(r, 0):
            copy.start()

    @pl.when(r + 1 < parts)
    def _():
        for copy in fetches(r + 1, (r + 1) % 2):
            copy.start()

    stores = []
    for s in range(slots):
        col = ((r + s) % parts) * rows
        for k in range(2):
            dst = outs[k].at[pl.ds(r * rows, rows), pl.ds(col, rows)]
            stores.append(pltpu.make_async_copy(g_ref.at[r, s, k], dst, sem_up.at[s, k]))
            stores[-1].start()
    slot = r % 2
    for copy in fetches(r, slot):
        copy.wait()
    for t in range(1, parts // 2):
        col = ((r + parts - t) % parts) * rows
        for k in range(2):
            flipped[t, k] = lower[slot, t, k].T
            dst = outs[k].at[pl.ds(r * rows, rows), pl.ds(col, rows)]
            stores.append(pltpu.make_async_copy(flipped.at[t, k], dst, sem_lo.at[t, k]))
            stores[-1].start()
    for copy in stores:
        copy.wait()


def assemble_pallas(chunks):
    (gathered,) = chunks
    parts, slots = gathered.shape[:2]
    rows = gathered.shape[-1]
    order = parts * rows
    return pl.pallas_call(
        assemble_kernel,
        grid=(parts,),
        in_specs=[pl.BlockSpec(memory_space=pl.ANY)],
        out_specs=[pl.BlockSpec(memory_space=pl.ANY)] * 2,
        out_shape=[jax.ShapeDtypeStruct((order, order), jnp.bfloat16)] * 2,
        scratch_shapes=[
            pltpu.VMEM((2, parts // 2, 2, rows, rows), jnp.bfloat16),
            pltpu.VMEM((parts // 2, 2, rows, rows), jnp.bfloat16),
            pltpu.SemaphoreType.DMA((2, parts // 2)),
            pltpu.SemaphoreType.DMA((slots, 2)),
            pltpu.SemaphoreType.DMA((parts // 2, 2)),
        ],
        compiler_params=pltpu.CompilerParams(dimension_semantics=("arbitrary",)),
    )(gathered)


def local(data_field, primary_field, station_weight, adaptive_filter, ring=None):
    rows = data_field.shape[1]
    order = data_field.shape[2]
    chips = lax.axis_size("chip")
    cores = lax.axis_size("core")
    parts = chips * cores
    here = lax.axis_index("chip") * cores + lax.axis_index("core")
    mine = jnp.concatenate(upper_blocks(data_field, station_weight, parts, here), axis=0)
    if ring is not None and cores == 2 and len(ring) * 2 == parts:
        gathered = [ring_gather(mine, ring, here)]
    else:
        gathered = [lax.all_gather(mine, AXES)]
    if rows % 128 == 0:
        operator = assemble_pallas(gathered)
    else:
        operator = assemble(jnp.concatenate(gathered, axis=1)[None], parts, 1)
    factor = 0.8 / math.sqrt(order)
    current = primary_field
    prediction = jnp.zeros(data_field.shape, jnp.float32)
    for step in range(ORDERS):
        stacked = current.reshape(2 * rows, order)
        with_real = jnp.dot(stacked, operator[0], preferred_element_type=jnp.float32)
        with_imag = jnp.dot(stacked, operator[1], preferred_element_type=jnp.float32)
        real_part = (with_real[:rows] - with_imag[rows:]) * factor
        imag_part = (with_imag[:rows] + with_real[rows:]) * factor
        current = jnp.stack([real_part, imag_part]).astype(jnp.bfloat16)
        prediction = prediction + current.astype(jnp.float32)
    filt_re = adaptive_filter[0][None, :]
    filt_im = adaptive_filter[1][None, :]
    out_re = data_field[0].astype(jnp.float32) - (filt_re * prediction[0] - filt_im * prediction[1])
    out_im = data_field[1].astype(jnp.float32) - (filt_re * prediction[1] + filt_im * prediction[0])
    return jnp.stack([out_re, out_im])


def solution(mesh):
    groups, parts = mesh.devices.shape
    split = Mesh(mesh.devices.reshape(groups, parts // 2, 2), ("grp",) + AXES)
    rows_spec = P(None, ("grp",) + AXES, None)
    try:
        ring = chip_ring(list(mesh.devices[0]))
    except (AttributeError, TypeError):
        ring = None
    return jax.shard_map(
        functools.partial(local, ring=ring),
        mesh=split,
        in_specs=(rows_spec, rows_spec, P(), P(None, "grp")),
        out_specs=rows_spec,
        check_vma=False,
    )
```

```python
import functools
import math

import numpy as np
import jax
import jax.numpy as jnp
from jax import lax
from jax.experimental import pallas as pl
from jax.experimental.pallas import tpu as pltpu
from jax.sharding import Mesh, PartitionSpec as P

ORDERS = 12
AXES = ("chip", "core")


def blend_rows(field, mirror, left_weight, right_weight):
    top = left_weight[:, None] * field.astype(jnp.float32) + right_weight[None, :] * mirror.astype(
        jnp.float32
    )
    return (top / (left_weight[:, None] + right_weight[None, :])).astype(jnp.bfloat16)


def upper_blocks(data_field, station_weight, parts, here):
    rows = data_field.shape[1]
    half = parts // 2
    rolled = jnp.roll(data_field.reshape(2, rows, parts, rows), -here, axis=2)
    own = rolled[:, :, : half + 1]
    received = [rolled[:, :, 0]]
    for s in range(1, half + 1):
        perm = [(c, (c - s) % parts) for c in range(parts)]
        received.append(lax.ppermute(rolled[:, :, parts - s], AXES, perm=perm))
    own_weight = lax.dynamic_slice_in_dim(station_weight, here * rows, rows)[:, None, None]
    col_weight = jnp.roll(station_weight.reshape(parts, rows), -here, axis=0)[None, : half + 1]
    chunks = []
    for lo, hi in chunk_bounds(half + 1):
        mirror = jnp.stack(received[lo:hi], axis=2).transpose(0, 3, 2, 1)
        top = own_weight * own[:, :, lo:hi].astype(jnp.float32) + col_weight[:, lo:hi] * mirror.astype(jnp.float32)
        blended = (top / (own_weight + col_weight[:, lo:hi])).astype(jnp.bfloat16)
        chunks.append(blended.transpose(2, 0, 1, 3))
    return chunks


def chunk_bounds(slots, pieces=3):
    edges = [round(i * slots / pieces) for i in range(pieces + 1)]
    return list(zip(edges[:-1], edges[1:]))


def assemble(gathered, chips, cores):
    parts = chips * cores
    slots = gathered.shape[2]
    rows = gathered.shape[-1]
    flat = gathered.reshape((parts, slots) + gathered.shape[3:])
    both = jnp.concatenate([flat, flat.swapaxes(-1, -2)], axis=1)
    where = lambda a: (a % cores) * chips + a // cores
    idx_a = np.zeros((parts, parts), np.int32)
    idx_s = np.zeros((parts, parts), np.int32)
    for r in range(parts):
        for c in range(parts):
            s = (c - r) % parts
            if s <= parts // 2:
                idx_a[r, c], idx_s[r, c] = where(r), s
            else:
                idx_a[r, c], idx_s[r, c] = where(c), slots + (r - c) % parts
    blocks = both[idx_a, idx_s]
    return blocks.transpose(2, 0, 3, 1, 4).reshape(2, parts * rows, parts * rows)


def chip_ring(devices):
    chips = list(devices[0::2])
    coords = [tuple(d.coords) for d in chips]
    axes = [i for i in range(3) if len({c[i] for c in coords}) > 1]
    if len(axes) == 1:
        return sorted(range(len(chips)), key=lambda h: coords[h][axes[0]])
    if len(axes) == 2:
        slow, fast = axes if len({c[axes[1]] for c in coords}) == 2 else axes[::-1]
        if len({c[fast] for c in coords}) == 2:
            lo, hi = sorted({c[fast] for c in coords})
            first = sorted((h for h in range(len(chips)) if coords[h][fast] == lo), key=lambda h: coords[h][slow])
            second = sorted((h for h in range(len(chips)) if coords[h][fast] == hi), key=lambda h: -coords[h][slow])
            return first + second
    return list(range(len(chips)))


def ring_gather(mine, ring, here):
    chips = len(ring)
    parts = 2 * chips
    core = here % 2
    chip = here // 2

    def ring_source(t):
        pick = 0
        for k, h in enumerate(ring):
            pick = pick + jnp.where(chip == h, ring[(k - t) % chips], 0)
        return pick

    ahead = [(ring[k] * 2 + c, ring[(k + 1) % chips] * 2 + c) for k in range(chips) for c in range(2)]
    behind = [(b, a) for a, b in ahead]
    sibling = [(a, a ^ 1) for a in range(parts)]
    out = pl.pallas_call(
        lambda ref: None,
        out_shape=jax.ShapeDtypeStruct((parts,) + mine.shape, mine.dtype),
        out_specs=pl.BlockSpec(memory_space=pl.ANY),
    )()
    out = lax.dynamic_update_slice(out, mine[None], (here, 0, 0, 0, 0))
    out = lax.dynamic_update_slice(out, lax.ppermute(mine, AXES, sibling)[None], (here ^ 1, 0, 0, 0, 0))
    fwd, back = mine[:, 0], mine[:, 1]
    for t in range(1, chips):
        fwd = lax.ppermute(fwd, AXES, ahead)
        back = lax.ppermute(back, AXES, behind)
        src_fwd = ring_source(t) * 2 + core
        src_back = ring_source(-t) * 2 + core
        out = lax.dynamic_update_slice(out, fwd[None, :, None], (src_fwd, 0, 0, 0, 0))
        out = lax.dynamic_update_slice(out, back[None, :, None], (src_back, 0, 1, 0, 0))
        out = lax.dynamic_update_slice(out, lax.ppermute(fwd, AXES, sibling)[None, :, None], (src_fwd ^ 1, 0, 0, 0, 0))
        out = lax.dynamic_update_slice(out, lax.ppermute(back, AXES, sibling)[None, :, None], (src_back ^ 1, 0, 1, 0, 0))
    return out


def assemble_kernel(*refs):
    pieces = len(refs) - 5
    g_refs, (re_ref, im_ref, upper, lower, sem) = refs[:pieces], refs[pieces:]
    parts = g_refs[0].shape[0]
    rows = g_refs[0].shape[-1]
    per = upper.shape[1]
    bounds = chunk_bounds(parts // 2 + 1, pieces)
    i = pl.program_id(0)

    def copies(step, slot):
        out = []
        for j in range(per):
            row = step * per + j
            for k, (lo, hi) in enumerate(bounds):
                dst = upper.at[slot, j, pl.ds(lo, hi - lo)]
                out.append(pltpu.make_async_copy(g_refs[k].at[row], dst, sem.at[slot, j, k]))
            for t in range(1, parts // 2):
                a = (row + parts - t) % parts
                k = [k for k, (lo, hi) in enumerate(bounds) if lo <= t < hi][0]
                src = g_refs[k].at[a, t - bounds[k][0]]
                out.append(pltpu.make_async_copy(src, lower.at[slot, j, t], sem.at[slot, j, pieces + t]))
        return out

    @pl.when(i == 0)
    def _():
        for copy in copies(i, 0):
            copy.start()

    @pl.when(i + 1 < parts // per)
    def _():
        for copy in copies(i + 1, (i + 1) % 2):
            copy.start()

    slot = i % 2
    for copy in copies(i, slot):
        copy.wait()
    for j in range(per):
        row = i * per + j
        for s in range(parts):
            col = pl.multiple_of(((row + s) % parts) * rows, rows)
            for k, out in ((0, re_ref), (1, im_ref)):
                if s <= parts // 2:
                    block = upper[slot, j, s, k]
                else:
                    block = lower[slot, j, parts - s, k].T
                out[j * rows:(j + 1) * rows, pl.ds(col, rows)] = block


def assemble_pallas(chunks, per=2):
    parts = chunks[0].shape[0]
    rows = chunks[0].shape[-1]
    slots = sum(c.shape[1] for c in chunks)
    order = parts * rows
    per = per if parts % per == 0 else 1
    return pl.pallas_call(
        assemble_kernel,
        grid=(parts // per,),
        in_specs=[pl.BlockSpec(memory_space=pl.ANY)] * len(chunks),
        out_specs=[pl.BlockSpec((per * rows, order), lambda i: (i, 0))] * 2,
        out_shape=[jax.ShapeDtypeStruct((order, order), jnp.bfloat16)] * 2,
        scratch_shapes=[
            pltpu.VMEM((2, per, slots, 2, rows, rows), jnp.bfloat16),
            pltpu.VMEM((2, per, parts // 2, 2, rows, rows), jnp.bfloat16),
            pltpu.SemaphoreType.DMA((2, per, len(chunks) + parts // 2)),
        ],
        compiler_params=pltpu.CompilerParams(dimension_semantics=("arbitrary",)),
    )(*chunks)


def local(data_field, primary_field, station_weight, adaptive_filter, ring=None):
    rows = data_field.shape[1]
    order = data_field.shape[2]
    chips = lax.axis_size("chip")
    cores = lax.axis_size("core")
    parts = chips * cores
    here = lax.axis_index("chip") * cores + lax.axis_index("core")
    mine = jnp.concatenate(upper_blocks(data_field, station_weight, parts, here), axis=0)
    if ring is not None and cores == 2 and len(ring) * 2 == parts:
        gathered = [ring_gather(mine, ring, here)]
    else:
        gathered = [lax.all_gather(mine, AXES)]
    if rows % 128 == 0:
        operator = assemble_pallas(gathered)
    else:
        operator = assemble(jnp.concatenate(gathered, axis=1)[None], parts, 1)
    factor = 0.8 / math.sqrt(order)
    current = primary_field
    prediction = jnp.zeros(data_field.shape, jnp.float32)
    for step in range(ORDERS):
        stacked = current.reshape(2 * rows, order)
        with_real = jnp.dot(stacked, operator[0], preferred_element_type=jnp.float32)
        with_imag = jnp.dot(stacked, operator[1], preferred_element_type=jnp.float32)
        real_part = (with_real[:rows] - with_imag[rows:]) * factor
        imag_part = (with_imag[:rows] + with_real[rows:]) * factor
        current = jnp.stack([real_part, imag_part]).astype(jnp.bfloat16)
        prediction = prediction + current.astype(jnp.float32)
    filt_re = adaptive_filter[0][None, :]
    filt_im = adaptive_filter[1][None, :]
    out_re = data_field[0].astype(jnp.float32) - (filt_re * prediction[0] - filt_im * prediction[1])
    out_im = data_field[1].astype(jnp.float32) - (filt_re * prediction[1] + filt_im * prediction[0])
    return jnp.stack([out_re, out_im])


def solution(mesh):
    groups, parts = mesh.devices.shape
    split = Mesh(mesh.devices.reshape(groups, parts // 2, 2), ("grp",) + AXES)
    rows_spec = P(None, ("grp",) + AXES, None)
    try:
        ring = chip_ring(list(mesh.devices[0]))
    except (AttributeError, TypeError):
        ring = None
    return jax.shard_map(
        functools.partial(local, ring=ring),
        mesh=split,
        in_specs=(rows_spec, rows_spec, P(), P(None, "grp")),
        out_specs=rows_spec,
        check_vma=False,
    )
```

```python
import functools
import math

import numpy as np
import jax
import jax.numpy as jnp
from jax import lax
from jax.experimental import pallas as pl
from jax.experimental.pallas import tpu as pltpu
from jax.sharding import Mesh, PartitionSpec as P

ORDERS = 12
AXES = ("chip", "core")


def blend_rows(field, mirror, left_weight, right_weight):
    top = left_weight[:, None] * field.astype(jnp.float32) + right_weight[None, :] * mirror.astype(
        jnp.float32
    )
    return (top / (left_weight[:, None] + right_weight[None, :])).astype(jnp.bfloat16)


def upper_blocks(data_field, station_weight, parts, here):
    rows = data_field.shape[1]
    half = parts // 2
    rolled = jnp.roll(data_field.reshape(2, rows, parts, rows), -here, axis=2)
    own = rolled[:, :, : half + 1]
    received = [rolled[:, :, 0]]
    for s in range(1, half + 1):
        perm = [(c, (c - s) % parts) for c in range(parts)]
        received.append(lax.ppermute(rolled[:, :, parts - s], AXES, perm=perm))
    own_weight = lax.dynamic_slice_in_dim(station_weight, here * rows, rows)[:, None, None]
    col_weight = jnp.roll(station_weight.reshape(parts, rows), -here, axis=0)[None, : half + 1]
    chunks = []
    for lo, hi in chunk_bounds(half + 1):
        mirror = jnp.stack(received[lo:hi], axis=2).transpose(0, 3, 2, 1)
        top = own_weight * own[:, :, lo:hi].astype(jnp.float32) + col_weight[:, lo:hi] * mirror.astype(jnp.float32)
        blended = (top / (own_weight + col_weight[:, lo:hi])).astype(jnp.bfloat16)
        chunks.append(blended.transpose(2, 0, 1, 3))
    return chunks


def chunk_bounds(slots, pieces=3):
    edges = [round(i * slots / pieces) for i in range(pieces + 1)]
    return list(zip(edges[:-1], edges[1:]))


def assemble(gathered, chips, cores):
    parts = chips * cores
    slots = gathered.shape[2]
    rows = gathered.shape[-1]
    flat = gathered.reshape((parts, slots) + gathered.shape[3:])
    both = jnp.concatenate([flat, flat.swapaxes(-1, -2)], axis=1)
    where = lambda a: (a % cores) * chips + a // cores
    idx_a = np.zeros((parts, parts), np.int32)
    idx_s = np.zeros((parts, parts), np.int32)
    for r in range(parts):
        for c in range(parts):
            s = (c - r) % parts
            if s <= parts // 2:
                idx_a[r, c], idx_s[r, c] = where(r), s
            else:
                idx_a[r, c], idx_s[r, c] = where(c), slots + (r - c) % parts
    blocks = both[idx_a, idx_s]
    return blocks.transpose(2, 0, 3, 1, 4).reshape(2, parts * rows, parts * rows)


def chip_ring(devices):
    chips = list(devices[0::2])
    coords = [tuple(d.coords) for d in chips]
    axes = [i for i in range(3) if len({c[i] for c in coords}) > 1]
    if len(axes) == 1:
        return sorted(range(len(chips)), key=lambda h: coords[h][axes[0]])
    if len(axes) == 2:
        slow, fast = axes if len({c[axes[1]] for c in coords}) == 2 else axes[::-1]
        if len({c[fast] for c in coords}) == 2:
            lo, hi = sorted({c[fast] for c in coords})
            first = sorted((h for h in range(len(chips)) if coords[h][fast] == lo), key=lambda h: coords[h][slow])
            second = sorted((h for h in range(len(chips)) if coords[h][fast] == hi), key=lambda h: -coords[h][slow])
            return first + second
    return list(range(len(chips)))


def ring_gather(mine, ring, here):
    chips = len(ring)
    parts = 2 * chips
    core = here % 2
    chip = here // 2

    def ring_source(t):
        pick = 0
        for k, h in enumerate(ring):
            pick = pick + jnp.where(chip == h, ring[(k - t) % chips], 0)
        return pick

    ahead = [(ring[k] * 2 + c, ring[(k + 1) % chips] * 2 + c) for k in range(chips) for c in range(2)]
    behind = [(b, a) for a, b in ahead]
    sibling = [(a, a ^ 1) for a in range(parts)]
    out = pl.pallas_call(
        lambda ref: None,
        out_shape=jax.ShapeDtypeStruct((parts,) + mine.shape, mine.dtype),
        out_specs=pl.BlockSpec(memory_space=pl.ANY),
    )()
    out = lax.dynamic_update_slice(out, mine[None], (here, 0, 0, 0, 0))
    out = lax.dynamic_update_slice(out, lax.ppermute(mine, AXES, sibling)[None], (here ^ 1, 0, 0, 0, 0))
    fwd, back = mine[:, 0], mine[:, 1]
    for t in range(1, chips):
        fwd = lax.ppermute(fwd, AXES, ahead)
        back = lax.ppermute(back, AXES, behind)
        src_fwd = ring_source(t) * 2 + core
        src_back = ring_source(-t) * 2 + core
        out = lax.dynamic_update_slice(out, fwd[None, :, None], (src_fwd, 0, 0, 0, 0))
        out = lax.dynamic_update_slice(out, back[None, :, None], (src_back, 0, 1, 0, 0))
        out = lax.dynamic_update_slice(out, lax.ppermute(fwd, AXES, sibling)[None, :, None], (src_fwd ^ 1, 0, 0, 0, 0))
        out = lax.dynamic_update_slice(out, lax.ppermute(back, AXES, sibling)[None, :, None], (src_back ^ 1, 0, 1, 0, 0))
    return out


def assemble_kernel(*refs):
    pieces = len(refs) - 5
    g_refs, (re_ref, im_ref, upper, lower, sem) = refs[:pieces], refs[pieces:]
    parts = g_refs[0].shape[0]
    rows = g_refs[0].shape[-1]
    per = upper.shape[1]
    bounds = chunk_bounds(parts // 2 + 1, pieces)
    i = pl.program_id(0)

    def copies(step, slot):
        out = []
        for j in range(per):
            row = step * per + j
            for k, (lo, hi) in enumerate(bounds):
                dst = upper.at[slot, j, pl.ds(lo, hi - lo)]
                out.append(pltpu.make_async_copy(g_refs[k].at[row], dst, sem.at[slot, j, k]))
            for t in range(1, parts // 2):
                a = (row + parts - t) % parts
                k = [k for k, (lo, hi) in enumerate(bounds) if lo <= t < hi][0]
                src = g_refs[k].at[a, t - bounds[k][0]]
                out.append(pltpu.make_async_copy(src, lower.at[slot, j, t], sem.at[slot, j, pieces + t]))
        return out

    @pl.when(i == 0)
    def _():
        for copy in copies(i, 0):
            copy.start()

    @pl.when(i + 1 < parts // per)
    def _():
        for copy in copies(i + 1, (i + 1) % 2):
            copy.start()

    slot = i % 2
    for copy in copies(i, slot):
        copy.wait()
    for j in range(per):
        row = i * per + j
        for s in range(parts):
            col = pl.multiple_of(((row + s) % parts) * rows, rows)
            for k, out in ((0, re_ref), (1, im_ref)):
                if s <= parts // 2:
                    block = upper[slot, j, s, k]
                else:
                    block = lower[slot, j, parts - s, k].T
                out[j * rows:(j + 1) * rows, pl.ds(col, rows)] = block


def assemble_pallas(chunks, per=4):
    parts = chunks[0].shape[0]
    rows = chunks[0].shape[-1]
    slots = sum(c.shape[1] for c in chunks)
    order = parts * rows
    per = per if parts % per == 0 else 1
    return pl.pallas_call(
        assemble_kernel,
        grid=(parts // per,),
        in_specs=[pl.BlockSpec(memory_space=pl.ANY)] * len(chunks),
        out_specs=[pl.BlockSpec((per * rows, order), lambda i: (i, 0))] * 2,
        out_shape=[jax.ShapeDtypeStruct((order, order), jnp.bfloat16)] * 2,
        scratch_shapes=[
            pltpu.VMEM((2, per, slots, 2, rows, rows), jnp.bfloat16),
            pltpu.VMEM((2, per, parts // 2, 2, rows, rows), jnp.bfloat16),
            pltpu.SemaphoreType.DMA((2, per, len(chunks) + parts // 2)),
        ],
        compiler_params=pltpu.CompilerParams(dimension_semantics=("arbitrary",)),
    )(*chunks)


def local(data_field, primary_field, station_weight, adaptive_filter, ring=None):
    rows = data_field.shape[1]
    order = data_field.shape[2]
    chips = lax.axis_size("chip")
    cores = lax.axis_size("core")
    parts = chips * cores
    here = lax.axis_index("chip") * cores + lax.axis_index("core")
    mine = jnp.concatenate(upper_blocks(data_field, station_weight, parts, here), axis=0)
    if ring is not None and cores == 2 and len(ring) * 2 == parts:
        gathered = [ring_gather(mine, ring, here)]
    else:
        gathered = [lax.all_gather(mine, AXES)]
    if rows % 128 == 0:
        operator = assemble_pallas(gathered)
    else:
        operator = assemble(jnp.concatenate(gathered, axis=1)[None], parts, 1)
    factor = 0.8 / math.sqrt(order)
    current = primary_field
    prediction = jnp.zeros(data_field.shape, jnp.float32)
    for step in range(ORDERS):
        stacked = current.reshape(2 * rows, order)
        with_real = jnp.dot(stacked, operator[0], preferred_element_type=jnp.float32)
        with_imag = jnp.dot(stacked, operator[1], preferred_element_type=jnp.float32)
        real_part = (with_real[:rows] - with_imag[rows:]) * factor
        imag_part = (with_imag[:rows] + with_real[rows:]) * factor
        current = jnp.stack([real_part, imag_part]).astype(jnp.bfloat16)
        prediction = prediction + current.astype(jnp.float32)
    filt_re = adaptive_filter[0][None, :]
    filt_im = adaptive_filter[1][None, :]
    out_re = data_field[0].astype(jnp.float32) - (filt_re * prediction[0] - filt_im * prediction[1])
    out_im = data_field[1].astype(jnp.float32) - (filt_re * prediction[1] + filt_im * prediction[0])
    return jnp.stack([out_re, out_im])


def solution(mesh):
    groups, parts = mesh.devices.shape
    split = Mesh(mesh.devices.reshape(groups, parts // 2, 2), ("grp",) + AXES)
    rows_spec = P(None, ("grp",) + AXES, None)
    try:
        ring = chip_ring(list(mesh.devices[0]))
    except (AttributeError, TypeError):
        ring = None
    return jax.shard_map(
        functools.partial(local, ring=ring),
        mesh=split,
        in_specs=(rows_spec, rows_spec, P(), P(None, "grp")),
        out_specs=rows_spec,
        check_vma=False,
    )
```

```python
import functools
import math

import numpy as np
import jax
import jax.numpy as jnp
from jax import lax
from jax.experimental import pallas as pl
from jax.experimental.pallas import tpu as pltpu
from jax.sharding import Mesh, PartitionSpec as P

ORDERS = 12
AXES = ("chip", "core")


def blend_rows(field, mirror, left_weight, right_weight):
    top = left_weight[:, None] * field.astype(jnp.float32) + right_weight[None, :] * mirror.astype(
        jnp.float32
    )
    return (top / (left_weight[:, None] + right_weight[None, :])).astype(jnp.bfloat16)


def upper_blocks(data_field, station_weight, parts, here):
    rows = data_field.shape[1]
    half = parts // 2
    rolled = jnp.roll(data_field.reshape(2, rows, parts, rows), -here, axis=2)
    own = rolled[:, :, : half + 1]
    received = [rolled[:, :, 0]]
    for s in range(1, half + 1):
        perm = [(c, (c - s) % parts) for c in range(parts)]
        received.append(lax.ppermute(rolled[:, :, parts - s], AXES, perm=perm))
    own_weight = lax.dynamic_slice_in_dim(station_weight, here * rows, rows)[:, None, None]
    col_weight = jnp.roll(station_weight.reshape(parts, rows), -here, axis=0)[None, : half + 1]
    chunks = []
    for lo, hi in chunk_bounds(half + 1):
        mirror = jnp.stack(received[lo:hi], axis=2).transpose(0, 3, 2, 1)
        top = own_weight * own[:, :, lo:hi].astype(jnp.float32) + col_weight[:, lo:hi] * mirror.astype(jnp.float32)
        blended = (top / (own_weight + col_weight[:, lo:hi])).astype(jnp.bfloat16)
        chunks.append(blended.transpose(2, 0, 1, 3))
    return chunks


def chunk_bounds(slots, pieces=3):
    edges = [round(i * slots / pieces) for i in range(pieces + 1)]
    return list(zip(edges[:-1], edges[1:]))


def assemble(gathered, chips, cores):
    parts = chips * cores
    slots = gathered.shape[2]
    rows = gathered.shape[-1]
    flat = gathered.reshape((parts, slots) + gathered.shape[3:])
    both = jnp.concatenate([flat, flat.swapaxes(-1, -2)], axis=1)
    where = lambda a: (a % cores) * chips + a // cores
    idx_a = np.zeros((parts, parts), np.int32)
    idx_s = np.zeros((parts, parts), np.int32)
    for r in range(parts):
        for c in range(parts):
            s = (c - r) % parts
            if s <= parts // 2:
                idx_a[r, c], idx_s[r, c] = where(r), s
            else:
                idx_a[r, c], idx_s[r, c] = where(c), slots + (r - c) % parts
    blocks = both[idx_a, idx_s]
    return blocks.transpose(2, 0, 3, 1, 4).reshape(2, parts * rows, parts * rows)


def chip_ring(devices):
    chips = list(devices[0::2])
    coords = [tuple(d.coords) for d in chips]
    axes = [i for i in range(3) if len({c[i] for c in coords}) > 1]
    if len(axes) == 1:
        return sorted(range(len(chips)), key=lambda h: coords[h][axes[0]])
    if len(axes) == 2:
        slow, fast = axes if len({c[axes[1]] for c in coords}) == 2 else axes[::-1]
        if len({c[fast] for c in coords}) == 2:
            lo, hi = sorted({c[fast] for c in coords})
            first = sorted((h for h in range(len(chips)) if coords[h][fast] == lo), key=lambda h: coords[h][slow])
            second = sorted((h for h in range(len(chips)) if coords[h][fast] == hi), key=lambda h: -coords[h][slow])
            return first + second
    return list(range(len(chips)))


def ring_gather(mine, ring, here):
    chips = len(ring)
    parts = 2 * chips
    core = here % 2
    chip = here // 2

    def ring_source(t):
        pick = 0
        for k, h in enumerate(ring):
            pick = pick + jnp.where(chip == h, ring[(k - t) % chips], 0)
        return pick

    ahead = [(ring[k] * 2 + c, ring[(k + 1) % chips] * 2 + c) for k in range(chips) for c in range(2)]
    behind = [(b, a) for a, b in ahead]
    sibling = [(a, a ^ 1) for a in range(parts)]
    out = pl.pallas_call(
        lambda ref: None,
        out_shape=jax.ShapeDtypeStruct((parts,) + mine.shape, mine.dtype),
        out_specs=pl.BlockSpec(memory_space=pl.ANY),
    )()
    out = lax.dynamic_update_slice(out, mine[None], (here, 0, 0, 0, 0))
    out = lax.dynamic_update_slice(out, lax.ppermute(mine, AXES, sibling)[None], (here ^ 1, 0, 0, 0, 0))
    fwd, back = mine[:, 0], mine[:, 1]
    for t in range(1, chips):
        fwd = lax.ppermute(fwd, AXES, ahead)
        back = lax.ppermute(back, AXES, behind)
        src_fwd = ring_source(t) * 2 + core
        src_back = ring_source(-t) * 2 + core
        out = lax.dynamic_update_slice(out, fwd[None, :, None], (src_fwd, 0, 0, 0, 0))
        out = lax.dynamic_update_slice(out, back[None, :, None], (src_back, 0, 1, 0, 0))
        out = lax.dynamic_update_slice(out, lax.ppermute(fwd, AXES, sibling)[None, :, None], (src_fwd ^ 1, 0, 0, 0, 0))
        out = lax.dynamic_update_slice(out, lax.ppermute(back, AXES, sibling)[None, :, None], (src_back ^ 1, 0, 1, 0, 0))
    return out


def assemble_kernel(*refs):
    pieces = len(refs) - 5
    g_refs, (re_ref, im_ref, upper, lower, sem) = refs[:pieces], refs[pieces:]
    parts = g_refs[0].shape[0]
    rows = g_refs[0].shape[-1]
    per = upper.shape[1]
    bounds = chunk_bounds(parts // 2 + 1, pieces)
    i = pl.program_id(0)

    def copies(step, slot):
        out = []
        for j in range(per):
            row = step * per + j
            for k, (lo, hi) in enumerate(bounds):
                dst = upper.at[slot, j, pl.ds(lo, hi - lo)]
                out.append(pltpu.make_async_copy(g_refs[k].at[row], dst, sem.at[slot, j, k]))
            for t in range(1, parts // 2):
                a = (row + parts - t) % parts
                k = [k for k, (lo, hi) in enumerate(bounds) if lo <= t < hi][0]
                src = g_refs[k].at[a, t - bounds[k][0]]
                out.append(pltpu.make_async_copy(src, lower.at[slot, j, t], sem.at[slot, j, pieces + t]))
        return out

    @pl.when(i == 0)
    def _():
        for copy in copies(i, 0):
            copy.start()

    @pl.when(i + 1 < parts // per)
    def _():
        for copy in copies(i + 1, (i + 1) % 2):
            copy.start()

    slot = i % 2
    for copy in copies(i, slot):
        copy.wait()
    for j in range(per):
        row = i * per + j
        for s in range(parts):
            col = pl.multiple_of(((row + s) % parts) * rows, rows)
            for k, out in ((0, re_ref), (1, im_ref)):
                if s <= parts // 2:
                    block = upper[slot, j, s, k]
                else:
                    block = lower[slot, j, parts - s, k].T
                out[j * rows:(j + 1) * rows, pl.ds(col, rows)] = block


def assemble_pallas(chunks, per=8):
    parts = chunks[0].shape[0]
    rows = chunks[0].shape[-1]
    slots = sum(c.shape[1] for c in chunks)
    order = parts * rows
    per = per if parts % per == 0 else 1
    return pl.pallas_call(
        assemble_kernel,
        grid=(parts // per,),
        in_specs=[pl.BlockSpec(memory_space=pl.ANY)] * len(chunks),
        out_specs=[pl.BlockSpec((per * rows, order), lambda i: (i, 0))] * 2,
        out_shape=[jax.ShapeDtypeStruct((order, order), jnp.bfloat16)] * 2,
        scratch_shapes=[
            pltpu.VMEM((2, per, slots, 2, rows, rows), jnp.bfloat16),
            pltpu.VMEM((2, per, parts // 2, 2, rows, rows), jnp.bfloat16),
            pltpu.SemaphoreType.DMA((2, per, len(chunks) + parts // 2)),
        ],
        compiler_params=pltpu.CompilerParams(dimension_semantics=("arbitrary",)),
    )(*chunks)


def local(data_field, primary_field, station_weight, adaptive_filter, ring=None):
    rows = data_field.shape[1]
    order = data_field.shape[2]
    chips = lax.axis_size("chip")
    cores = lax.axis_size("core")
    parts = chips * cores
    here = lax.axis_index("chip") * cores + lax.axis_index("core")
    mine = jnp.concatenate(upper_blocks(data_field, station_weight, parts, here), axis=0)
    if ring is not None and cores == 2 and len(ring) * 2 == parts:
        gathered = [ring_gather(mine, ring, here)]
    else:
        gathered = [lax.all_gather(mine, AXES)]
    if rows % 128 == 0:
        operator = assemble_pallas(gathered)
    else:
        operator = assemble(jnp.concatenate(gathered, axis=1)[None], parts, 1)
    factor = 0.8 / math.sqrt(order)
    current = primary_field
    prediction = jnp.zeros(data_field.shape, jnp.float32)
    for step in range(ORDERS):
        stacked = current.reshape(2 * rows, order)
        with_real = jnp.dot(stacked, operator[0], preferred_element_type=jnp.float32)
        with_imag = jnp.dot(stacked, operator[1], preferred_element_type=jnp.float32)
        real_part = (with_real[:rows] - with_imag[rows:]) * factor
        imag_part = (with_imag[:rows] + with_real[rows:]) * factor
        current = jnp.stack([real_part, imag_part]).astype(jnp.bfloat16)
        prediction = prediction + current.astype(jnp.float32)
    filt_re = adaptive_filter[0][None, :]
    filt_im = adaptive_filter[1][None, :]
    out_re = data_field[0].astype(jnp.float32) - (filt_re * prediction[0] - filt_im * prediction[1])
    out_im = data_field[1].astype(jnp.float32) - (filt_re * prediction[1] + filt_im * prediction[0])
    return jnp.stack([out_re, out_im])


def solution(mesh):
    groups, parts = mesh.devices.shape
    split = Mesh(mesh.devices.reshape(groups, parts // 2, 2), ("grp",) + AXES)
    rows_spec = P(None, ("grp",) + AXES, None)
    try:
        ring = chip_ring(list(mesh.devices[0]))
    except (AttributeError, TypeError):
        ring = None
    return jax.shard_map(
        functools.partial(local, ring=ring),
        mesh=split,
        in_specs=(rows_spec, rows_spec, P(), P(None, "grp")),
        out_specs=rows_spec,
        check_vma=False,
    )
```

```python
import functools
import math

import numpy as np
import jax
import jax.numpy as jnp
from jax import lax
from jax.experimental import pallas as pl
from jax.experimental.pallas import tpu as pltpu
from jax.sharding import Mesh, PartitionSpec as P

ORDERS = 12
AXES = ("chip", "core")


def blend_rows(field, mirror, left_weight, right_weight):
    top = left_weight[:, None] * field.astype(jnp.float32) + right_weight[None, :] * mirror.astype(
        jnp.float32
    )
    return (top / (left_weight[:, None] + right_weight[None, :])).astype(jnp.bfloat16)


def upper_blocks(data_field, station_weight, parts, here):
    rows = data_field.shape[1]
    half = parts // 2
    rolled = jnp.roll(data_field.reshape(2, rows, parts, rows), -here, axis=2)
    own = rolled[:, :, : half + 1]
    received = [rolled[:, :, 0]]
    for s in range(1, half + 1):
        perm = [(c, (c - s) % parts) for c in range(parts)]
        received.append(lax.ppermute(rolled[:, :, parts - s], AXES, perm=perm))
    own_weight = lax.dynamic_slice_in_dim(station_weight, here * rows, rows)[:, None, None]
    col_weight = jnp.roll(station_weight.reshape(parts, rows), -here, axis=0)[None, : half + 1]
    chunks = []
    for lo, hi in chunk_bounds(half + 1):
        mirror = jnp.stack(received[lo:hi], axis=2).transpose(0, 3, 2, 1)
        top = own_weight * own[:, :, lo:hi].astype(jnp.float32) + col_weight[:, lo:hi] * mirror.astype(jnp.float32)
        blended = (top / (own_weight + col_weight[:, lo:hi])).astype(jnp.bfloat16)
        chunks.append(blended.transpose(2, 0, 1, 3))
    return chunks


def chunk_bounds(slots, pieces=3):
    edges = [round(i * slots / pieces) for i in range(pieces + 1)]
    return list(zip(edges[:-1], edges[1:]))


def assemble(gathered, chips, cores):
    parts = chips * cores
    slots = gathered.shape[2]
    rows = gathered.shape[-1]
    flat = gathered.reshape((parts, slots) + gathered.shape[3:])
    both = jnp.concatenate([flat, flat.swapaxes(-1, -2)], axis=1)
    where = lambda a: (a % cores) * chips + a // cores
    idx_a = np.zeros((parts, parts), np.int32)
    idx_s = np.zeros((parts, parts), np.int32)
    for r in range(parts):
        for c in range(parts):
            s = (c - r) % parts
            if s <= parts // 2:
                idx_a[r, c], idx_s[r, c] = where(r), s
            else:
                idx_a[r, c], idx_s[r, c] = where(c), slots + (r - c) % parts
    blocks = both[idx_a, idx_s]
    return blocks.transpose(2, 0, 3, 1, 4).reshape(2, parts * rows, parts * rows)


def chip_ring(devices):
    chips = list(devices[0::2])
    coords = [tuple(d.coords) for d in chips]
    axes = [i for i in range(3) if len({c[i] for c in coords}) > 1]
    if len(axes) == 1:
        return sorted(range(len(chips)), key=lambda h: coords[h][axes[0]])
    if len(axes) == 2:
        slow, fast = axes if len({c[axes[1]] for c in coords}) == 2 else axes[::-1]
        if len({c[fast] for c in coords}) == 2:
            lo, hi = sorted({c[fast] for c in coords})
            first = sorted((h for h in range(len(chips)) if coords[h][fast] == lo), key=lambda h: coords[h][slow])
            second = sorted((h for h in range(len(chips)) if coords[h][fast] == hi), key=lambda h: -coords[h][slow])
            return first + second
    return list(range(len(chips)))


def ring_gather(mine, ring, here):
    chips = len(ring)
    parts = 2 * chips
    core = here % 2
    chip = here // 2

    def ring_source(t):
        pick = 0
        for k, h in enumerate(ring):
            pick = pick + jnp.where(chip == h, ring[(k - t) % chips], 0)
        return pick

    ahead = [(ring[k] * 2 + c, ring[(k + 1) % chips] * 2 + c) for k in range(chips) for c in range(2)]
    behind = [(b, a) for a, b in ahead]
    sibling = [(a, a ^ 1) for a in range(parts)]
    out = pl.pallas_call(
        lambda ref: None,
        out_shape=jax.ShapeDtypeStruct((parts,) + mine.shape, mine.dtype),
        out_specs=pl.BlockSpec(memory_space=pl.ANY),
    )()
    out = lax.dynamic_update_slice(out, mine[None], (here, 0, 0, 0, 0))
    shard = lax.ppermute(mine, AXES, sibling)
    fwd, back = mine[:, 0], mine[:, 1]
    for t in range(1, chips):
        fwd = lax.ppermute(fwd, AXES, ahead)
        back = lax.ppermute(back, AXES, behind)
        src_fwd = ring_source(t) * 2 + core
        src_back = ring_source(-t) * 2 + core
        out = lax.dynamic_update_slice(out, fwd[None, :, None], (src_fwd, 0, 0, 0, 0))
        out = lax.dynamic_update_slice(out, back[None, :, None], (src_back, 0, 1, 0, 0))
        out = lax.dynamic_update_slice(out, lax.ppermute(fwd, AXES, sibling)[None, :, None], (src_fwd ^ 1, 0, 0, 0, 0))
        out = lax.dynamic_update_slice(out, lax.ppermute(back, AXES, sibling)[None, :, None], (src_back ^ 1, 0, 1, 0, 0))
    return lax.dynamic_update_slice(out, shard[None], (here ^ 1, 0, 0, 0, 0))


def assemble_kernel(*refs):
    pieces = len(refs) - 5
    g_refs, (re_ref, im_ref, upper, lower, sem) = refs[:pieces], refs[pieces:]
    parts = g_refs[0].shape[0]
    rows = g_refs[0].shape[-1]
    per = upper.shape[1]
    bounds = chunk_bounds(parts // 2 + 1, pieces)
    i = pl.program_id(0)

    def copies(step, slot):
        out = []
        for j in range(per):
            row = step * per + j
            for k, (lo, hi) in enumerate(bounds):
                dst = upper.at[slot, j, pl.ds(lo, hi - lo)]
                out.append(pltpu.make_async_copy(g_refs[k].at[row], dst, sem.at[slot, j, k]))
            for t in range(1, parts // 2):
                a = (row + parts - t) % parts
                k = [k for k, (lo, hi) in enumerate(bounds) if lo <= t < hi][0]
                src = g_refs[k].at[a, t - bounds[k][0]]
                out.append(pltpu.make_async_copy(src, lower.at[slot, j, t], sem.at[slot, j, pieces + t]))
        return out

    @pl.when(i == 0)
    def _():
        for copy in copies(i, 0):
            copy.start()

    @pl.when(i + 1 < parts // per)
    def _():
        for copy in copies(i + 1, (i + 1) % 2):
            copy.start()

    slot = i % 2
    for copy in copies(i, slot):
        copy.wait()
    for j in range(per):
        row = i * per + j
        for s in range(parts):
            col = pl.multiple_of(((row + s) % parts) * rows, rows)
            for k, out in ((0, re_ref), (1, im_ref)):
                if s <= parts // 2:
                    block = upper[slot, j, s, k]
                else:
                    block = lower[slot, j, parts - s, k].T
                out[j * rows:(j + 1) * rows, pl.ds(col, rows)] = block


def assemble_pallas(chunks, per=4):
    parts = chunks[0].shape[0]
    rows = chunks[0].shape[-1]
    slots = sum(c.shape[1] for c in chunks)
    order = parts * rows
    per = per if parts % per == 0 else 1
    return pl.pallas_call(
        assemble_kernel,
        grid=(parts // per,),
        in_specs=[pl.BlockSpec(memory_space=pl.ANY)] * len(chunks),
        out_specs=[pl.BlockSpec((per * rows, order), lambda i: (i, 0))] * 2,
        out_shape=[jax.ShapeDtypeStruct((order, order), jnp.bfloat16)] * 2,
        scratch_shapes=[
            pltpu.VMEM((2, per, slots, 2, rows, rows), jnp.bfloat16),
            pltpu.VMEM((2, per, parts // 2, 2, rows, rows), jnp.bfloat16),
            pltpu.SemaphoreType.DMA((2, per, len(chunks) + parts // 2)),
        ],
        compiler_params=pltpu.CompilerParams(dimension_semantics=("arbitrary",)),
    )(*chunks)


def local(data_field, primary_field, station_weight, adaptive_filter, ring=None):
    rows = data_field.shape[1]
    order = data_field.shape[2]
    chips = lax.axis_size("chip")
    cores = lax.axis_size("core")
    parts = chips * cores
    here = lax.axis_index("chip") * cores + lax.axis_index("core")
    mine = jnp.concatenate(upper_blocks(data_field, station_weight, parts, here), axis=0)
    if ring is not None and cores == 2 and len(ring) * 2 == parts:
        gathered = [ring_gather(mine, ring, here)]
    else:
        gathered = [lax.all_gather(mine, AXES)]
    if rows % 128 == 0:
        operator = assemble_pallas(gathered)
    else:
        operator = assemble(jnp.concatenate(gathered, axis=1)[None], parts, 1)
    factor = 0.8 / math.sqrt(order)
    current = primary_field
    prediction = jnp.zeros(data_field.shape, jnp.float32)
    for step in range(ORDERS):
        stacked = current.reshape(2 * rows, order)
        with_real = jnp.dot(stacked, operator[0], preferred_element_type=jnp.float32)
        with_imag = jnp.dot(stacked, operator[1], preferred_element_type=jnp.float32)
        real_part = (with_real[:rows] - with_imag[rows:]) * factor
        imag_part = (with_imag[:rows] + with_real[rows:]) * factor
        current = jnp.stack([real_part, imag_part]).astype(jnp.bfloat16)
        prediction = prediction + current.astype(jnp.float32)
    filt_re = adaptive_filter[0][None, :]
    filt_im = adaptive_filter[1][None, :]
    out_re = data_field[0].astype(jnp.float32) - (filt_re * prediction[0] - filt_im * prediction[1])
    out_im = data_field[1].astype(jnp.float32) - (filt_re * prediction[1] + filt_im * prediction[0])
    return jnp.stack([out_re, out_im])


def solution(mesh):
    groups, parts = mesh.devices.shape
    split = Mesh(mesh.devices.reshape(groups, parts // 2, 2), ("grp",) + AXES)
    rows_spec = P(None, ("grp",) + AXES, None)
    try:
        ring = chip_ring(list(mesh.devices[0]))
    except (AttributeError, TypeError):
        ring = None
    return jax.shard_map(
        functools.partial(local, ring=ring),
        mesh=split,
        in_specs=(rows_spec, rows_spec, P(), P(None, "grp")),
        out_specs=rows_spec,
        check_vma=False,
    )
```

```python
import functools
import math

import numpy as np
import jax
import jax.numpy as jnp
from jax import lax
from jax.experimental import pallas as pl
from jax.experimental.pallas import tpu as pltpu
from jax.sharding import Mesh, PartitionSpec as P

ORDERS = 12
AXES = ("chip", "core")


def blend_rows(field, mirror, left_weight, right_weight):
    top = left_weight[:, None] * field.astype(jnp.float32) + right_weight[None, :] * mirror.astype(
        jnp.float32
    )
    return (top / (left_weight[:, None] + right_weight[None, :])).astype(jnp.bfloat16)


def upper_blocks(data_field, station_weight, parts, here):
    rows = data_field.shape[1]
    half = parts // 2
    rolled = jnp.roll(data_field.reshape(2, rows, parts, rows), -here, axis=2)
    own = rolled[:, :, : half + 1]
    received = [rolled[:, :, 0]]
    for s in range(1, half + 1):
        perm = [(c, (c - s) % parts) for c in range(parts)]
        received.append(lax.ppermute(rolled[:, :, parts - s], AXES, perm=perm))
    own_weight = lax.dynamic_slice_in_dim(station_weight, here * rows, rows)[:, None, None]
    col_weight = jnp.roll(station_weight.reshape(parts, rows), -here, axis=0)[None, : half + 1]
    chunks = []
    for lo, hi in chunk_bounds(half + 1, half + 1):
        mirror = jnp.stack(received[lo:hi], axis=2).transpose(0, 3, 2, 1)
        top = own_weight * own[:, :, lo:hi].astype(jnp.float32) + col_weight[:, lo:hi] * mirror.astype(jnp.float32)
        blended = (top / (own_weight + col_weight[:, lo:hi])).astype(jnp.bfloat16)
        chunks.append(blended.transpose(2, 0, 1, 3))
    return chunks


def chunk_bounds(slots, pieces=3):
    edges = [round(i * slots / pieces) for i in range(pieces + 1)]
    return list(zip(edges[:-1], edges[1:]))


def assemble(gathered, chips, cores):
    parts = chips * cores
    slots = gathered.shape[2]
    rows = gathered.shape[-1]
    flat = gathered.reshape((parts, slots) + gathered.shape[3:])
    both = jnp.concatenate([flat, flat.swapaxes(-1, -2)], axis=1)
    where = lambda a: (a % cores) * chips + a // cores
    idx_a = np.zeros((parts, parts), np.int32)
    idx_s = np.zeros((parts, parts), np.int32)
    for r in range(parts):
        for c in range(parts):
            s = (c - r) % parts
            if s <= parts // 2:
                idx_a[r, c], idx_s[r, c] = where(r), s
            else:
                idx_a[r, c], idx_s[r, c] = where(c), slots + (r - c) % parts
    blocks = both[idx_a, idx_s]
    return blocks.transpose(2, 0, 3, 1, 4).reshape(2, parts * rows, parts * rows)


def chip_ring(devices):
    chips = list(devices[0::2])
    coords = [tuple(d.coords) for d in chips]
    axes = [i for i in range(3) if len({c[i] for c in coords}) > 1]
    if len(axes) == 1:
        return sorted(range(len(chips)), key=lambda h: coords[h][axes[0]])
    if len(axes) == 2:
        slow, fast = axes if len({c[axes[1]] for c in coords}) == 2 else axes[::-1]
        if len({c[fast] for c in coords}) == 2:
            lo, hi = sorted({c[fast] for c in coords})
            first = sorted((h for h in range(len(chips)) if coords[h][fast] == lo), key=lambda h: coords[h][slow])
            second = sorted((h for h in range(len(chips)) if coords[h][fast] == hi), key=lambda h: -coords[h][slow])
            return first + second
    return list(range(len(chips)))


def ring_gather(mine, ring, here):
    chips = len(ring)
    parts = 2 * chips
    core = here % 2
    chip = here // 2

    def ring_source(t):
        pick = 0
        for k, h in enumerate(ring):
            pick = pick + jnp.where(chip == h, ring[(k - t) % chips], 0)
        return pick

    ahead = [(ring[k] * 2 + c, ring[(k + 1) % chips] * 2 + c) for k in range(chips) for c in range(2)]
    behind = [(b, a) for a, b in ahead]
    sibling = [(a, a ^ 1) for a in range(parts)]
    out = pl.pallas_call(
        lambda ref: None,
        out_shape=jax.ShapeDtypeStruct((parts,) + mine.shape, mine.dtype),
        out_specs=pl.BlockSpec(memory_space=pl.ANY),
    )()
    out = lax.dynamic_update_slice(out, mine[None], (here, 0, 0, 0, 0))
    out = lax.dynamic_update_slice(out, lax.ppermute(mine, AXES, sibling)[None], (here ^ 1, 0, 0, 0, 0))
    fwd, back = mine[:, 0], mine[:, 1]
    for t in range(1, chips):
        fwd = lax.ppermute(fwd, AXES, ahead)
        back = lax.ppermute(back, AXES, behind)
        src_fwd = ring_source(t) * 2 + core
        src_back = ring_source(-t) * 2 + core
        out = lax.dynamic_update_slice(out, fwd[None, :, None], (src_fwd, 0, 0, 0, 0))
        out = lax.dynamic_update_slice(out, back[None, :, None], (src_back, 0, 1, 0, 0))
        out = lax.dynamic_update_slice(out, lax.ppermute(fwd, AXES, sibling)[None, :, None], (src_fwd ^ 1, 0, 0, 0, 0))
        out = lax.dynamic_update_slice(out, lax.ppermute(back, AXES, sibling)[None, :, None], (src_back ^ 1, 0, 1, 0, 0))
    return out


def assemble_kernel(*refs):
    pieces = len(refs) - 5
    g_refs, (re_ref, im_ref, upper, lower, sem) = refs[:pieces], refs[pieces:]
    parts = g_refs[0].shape[0]
    rows = g_refs[0].shape[-1]
    per = upper.shape[1]
    bounds = chunk_bounds(parts // 2 + 1, pieces)
    i = pl.program_id(0)

    def copies(step, slot):
        out = []
        for j in range(per):
            row = step * per + j
            for k, (lo, hi) in enumerate(bounds):
                dst = upper.at[slot, j, pl.ds(lo, hi - lo)]
                out.append(pltpu.make_async_copy(g_refs[k].at[row], dst, sem.at[slot, j, k]))
            for t in range(1, parts // 2):
                a = (row + parts - t) % parts
                k = [k for k, (lo, hi) in enumerate(bounds) if lo <= t < hi][0]
                src = g_refs[k].at[a, t - bounds[k][0]]
                out.append(pltpu.make_async_copy(src, lower.at[slot, j, t], sem.at[slot, j, pieces + t]))
        return out

    @pl.when(i == 0)
    def _():
        for copy in copies(i, 0):
            copy.start()

    @pl.when(i + 1 < parts // per)
    def _():
        for copy in copies(i + 1, (i + 1) % 2):
            copy.start()

    slot = i % 2
    for copy in copies(i, slot):
        copy.wait()
    for j in range(per):
        row = i * per + j
        for s in range(parts):
            col = pl.multiple_of(((row + s) % parts) * rows, rows)
            for k, out in ((0, re_ref), (1, im_ref)):
                if s <= parts // 2:
                    block = upper[slot, j, s, k]
                else:
                    block = lower[slot, j, parts - s, k].T
                out[j * rows:(j + 1) * rows, pl.ds(col, rows)] = block


def assemble_pallas(chunks, per=4):
    parts = chunks[0].shape[0]
    rows = chunks[0].shape[-1]
    slots = sum(c.shape[1] for c in chunks)
    order = parts * rows
    per = per if parts % per == 0 else 1
    return pl.pallas_call(
        assemble_kernel,
        grid=(parts // per,),
        in_specs=[pl.BlockSpec(memory_space=pl.ANY)] * len(chunks),
        out_specs=[pl.BlockSpec((per * rows, order), lambda i: (i, 0))] * 2,
        out_shape=[jax.ShapeDtypeStruct((order, order), jnp.bfloat16)] * 2,
        scratch_shapes=[
            pltpu.VMEM((2, per, slots, 2, rows, rows), jnp.bfloat16),
            pltpu.VMEM((2, per, parts // 2, 2, rows, rows), jnp.bfloat16),
            pltpu.SemaphoreType.DMA((2, per, len(chunks) + parts // 2)),
        ],
        compiler_params=pltpu.CompilerParams(dimension_semantics=("arbitrary",)),
    )(*chunks)


def local(data_field, primary_field, station_weight, adaptive_filter, ring=None):
    rows = data_field.shape[1]
    order = data_field.shape[2]
    chips = lax.axis_size("chip")
    cores = lax.axis_size("core")
    parts = chips * cores
    here = lax.axis_index("chip") * cores + lax.axis_index("core")
    mine = jnp.concatenate(upper_blocks(data_field, station_weight, parts, here), axis=0)
    if ring is not None and cores == 2 and len(ring) * 2 == parts:
        gathered = [ring_gather(mine, ring, here)]
    else:
        gathered = [lax.all_gather(mine, AXES)]
    if rows % 128 == 0:
        operator = assemble_pallas(gathered)
    else:
        operator = assemble(jnp.concatenate(gathered, axis=1)[None], parts, 1)
    factor = 0.8 / math.sqrt(order)
    current = primary_field
    prediction = jnp.zeros(data_field.shape, jnp.float32)
    for step in range(ORDERS):
        stacked = current.reshape(2 * rows, order)
        with_real = jnp.dot(stacked, operator[0], preferred_element_type=jnp.float32)
        with_imag = jnp.dot(stacked, operator[1], preferred_element_type=jnp.float32)
        real_part = (with_real[:rows] - with_imag[rows:]) * factor
        imag_part = (with_imag[:rows] + with_real[rows:]) * factor
        current = jnp.stack([real_part, imag_part]).astype(jnp.bfloat16)
        prediction = prediction + current.astype(jnp.float32)
    filt_re = adaptive_filter[0][None, :]
    filt_im = adaptive_filter[1][None, :]
    out_re = data_field[0].astype(jnp.float32) - (filt_re * prediction[0] - filt_im * prediction[1])
    out_im = data_field[1].astype(jnp.float32) - (filt_re * prediction[1] + filt_im * prediction[0])
    return jnp.stack([out_re, out_im])


def solution(mesh):
    groups, parts = mesh.devices.shape
    split = Mesh(mesh.devices.reshape(groups, parts // 2, 2), ("grp",) + AXES)
    rows_spec = P(None, ("grp",) + AXES, None)
    try:
        ring = chip_ring(list(mesh.devices[0]))
    except (AttributeError, TypeError):
        ring = None
    return jax.shard_map(
        functools.partial(local, ring=ring),
        mesh=split,
        in_specs=(rows_spec, rows_spec, P(), P(None, "grp")),
        out_specs=rows_spec,
        check_vma=False,
    )
```
